32 devices in a mesh: groups: 2 (over y), pts: 4 (over z), cam: 4 (over x, core).
Axes of the slice: x: 2, y: 2, z: 4, core: 2. Of those that a mesh axis runs over, the one named last changes fastest.
Arguments:
- cam_jac: float32 [2, 9, 131072], P(None, None, ('groups', 'pts', 'cam')), parts along dimension 2, may hold values from -0.4 to 0.4
- point_jac: float32 [2, 3, 131072], P(None, None, ('groups', 'pts', 'cam')), parts along dimension 2, may hold values from -3 to 3
- obs_cam: int32 [131072], P(('groups', 'pts', 'cam')), parts along dimension 0, may hold values from 0 to 511
- obs_point: int32 [131072], P(('groups', 'pts', 'cam')), parts along dimension 0, may hold values from 0 to 4095
- point_damp: float32 [32768], P(('groups', 'pts')), parts along dimension 0, may hold values from 0.5 to 4
- cam_damp: float32 [4096], P(('groups', 'cam')), parts along dimension 0, may hold values from 0.5 to 4
- reduced_rhs: float32 [9, 4096], P(None, ('groups', 'cam')), parts along dimension 1, may hold values from -6 to 6
Outputs:
- solution: float32 [9, 4096], P(None, ('groups', 'cam')), parts along dimension 1
- residual: float32 [9, 4096], P(None, ('groups', 'cam')), parts along dimension 1
The draws below stay inside these ranges and needn't reach their ends.
There are 2 independent parts, one for each index of `groups`. The reference program is written for one: setup_inputs(seed, part) draws one part's arguments, and reference() takes and returns one part's arrays. A program takes and returns all parts, laid end to end along the dimension named above; each array names one. Nothing has to cross between parts.
All inputs are finite; a program needn't handle non-finite values.
Results may differ from the reference program's by a relative error of at most 0.0003.
Values sent between devices are 32-bit elements; how exact they have to be, the bound alone decides.
No kernel may reach another device: no remote copies, remote signals or barrier semaphores. Data moves between devices by JAX's collectives and lax.ppermute only.
A program may use at most 64 MiB of HBM per device.

```python
import math
import jax
import jax.numpy as jnp
from jax import lax

CPAR = 9
CB = 512
PTS_DEV = 4096
OBS_DEV = 4096
ITERS = 3
NC = 2048
NP = 16384
NOBS = 65536
N_CAM = 4


def place_ends(array, stream_key, low, top_value):
    longest = array.shape.index(max(array.shape))
    spots = []
    for shift in (0, 1):
        where = [jax.random.randint(jax.random.fold_in(stream_key, axis), (), 0, length) for axis, length in enumerate(array.shape)]
        where[longest] = (where[longest] + shift) % array.shape[longest]
        spots.append(tuple(where))
    return array.at[spots[0]].set(low).at[spots[1]].set(top_value)


def block_scale(own_key, shape, split, smallest, high):
    loudness, own = 1.0, jax.random.fold_in(own_key, 6)
    for position, shards_of in split:
        draws = jnp.exp(jax.random.uniform(jax.random.fold_in(own, position), (shards_of,), jnp.float32, smallest / len(split), high / len(split)))
        loudness = loudness * jnp.repeat(draws, shape[position] // shards_of).reshape([-1 if axis == position else 1 for axis in range(len(shape))])
    return loudness


def gaussian(own_key, shape, scale, bound, cuts=(), held_as=jnp.bfloat16):
    result = jax.random.normal(own_key, shape, jnp.float32) * scale
    if len(cuts) > 0:
        result = block_scale(own_key, shape, cuts, -0.22, 0.18) * result
    return jnp.clip(result, min=-bound, max=bound).astype(held_as)


def setup_inputs(seed: int = 0, part: int = 0) -> dict:
    splits = jax.random.split(jax.random.key(seed), 8)
    own_keys = jax.random.split(jax.random.fold_in(splits[7], part), 8)
    cam_jac = gaussian(own_keys[0], (2, CPAR, NOBS), 0.05, 0.4, ((2, 16),), jnp.float32)
    point_jac = gaussian(own_keys[1], (2, 3, NOBS), 0.5, 3.0, ((2, 16),), jnp.float32)
    obs_cam = place_ends(jax.random.randint(own_keys[2], (NOBS,), 0, CB), jax.random.fold_in(own_keys[2], 1), 0, CB - 1).astype(jnp.int32)
    obs_point = place_ends(jax.random.randint(own_keys[3], (NOBS,), 0, PTS_DEV), jax.random.fold_in(own_keys[3], 1), 0, PTS_DEV - 1).astype(jnp.int32)
    point_damp = jnp.clip(jnp.exp(math.log(4.0) - 2.0794415 * jax.random.uniform(own_keys[4], (NP,), jnp.float32) ** block_scale(own_keys[4], (NP,), ((0, 4),), -0.2, 0.2)), 0.5, 4.0)
    cam_damp = jnp.clip(jnp.exp(math.log(4.0) - 2.0794415 * jax.random.uniform(own_keys[5], (NC,), jnp.float32) ** block_scale(own_keys[5], (NC,), ((0, 4),), -0.2, 0.2)), 0.5, 4.0)
    reduced_rhs = gaussian(own_keys[6], (CPAR, NC), 1.0, 6.0, ((1, 4),), jnp.float32)
    return dict(cam_jac=cam_jac, point_jac=point_jac, obs_cam=obs_cam, obs_point=obs_point, point_damp=point_damp, cam_damp=cam_damp, reduced_rhs=reduced_rhs)


HI = lax.Precision.HIGHEST


def segsum(terms, index, count):
    return jax.ops.segment_sum(terms.T, index, num_segments=count).T


def invert3(mat):
    a = mat
    c00 = a[1, 1] * a[2, 2] - a[1, 2] * a[2, 1]
    c01 = a[0, 2] * a[2, 1] - a[0, 1] * a[2, 2]
    c02 = a[0, 1] * a[1, 2] - a[0, 2] * a[1, 1]
    c10 = a[1, 2] * a[2, 0] - a[1, 0] * a[2, 2]
    c11 = a[0, 0] * a[2, 2] - a[0, 2] * a[2, 0]
    c12 = a[0, 2] * a[1, 0] - a[0, 0] * a[1, 2]
    c20 = a[1, 0] * a[2, 1] - a[1, 1] * a[2, 0]
    c21 = a[0, 1] * a[2, 0] - a[0, 0] * a[2, 1]
    c22 = a[0, 0] * a[1, 1] - a[0, 1] * a[1, 0]
    det = a[0, 0] * c00 + a[0, 1] * c10 + a[0, 2] * c20
    adj = jnp.stack([jnp.stack([c00, c01, c02]), jnp.stack([c10, c11, c12]), jnp.stack([c20, c21, c22])])
    return adj / det


def point_matrix(point_jac, point_idx, count):
    terms = jnp.einsum("rao,rbo->abo", point_jac, point_jac, precision=HI)
    return segsum(terms.reshape(9, -1), point_idx, count).reshape(3, 3, count)


def camera_diag_terms(cam_jac, cam_idx, count):
    return segsum(jnp.sum(cam_jac * cam_jac, axis=0), cam_idx, count)


def reference(cam_jac, point_jac, obs_cam, obs_point, point_damp, cam_damp, reduced_rhs):
    nobs = obs_cam.shape[0]
    block = jnp.arange(nobs, dtype=jnp.int32) // OBS_DEV
    cam_idx = (block % N_CAM) * CB + obs_cam
    point_idx = (block // N_CAM) * PTS_DEV + obs_point
    ncam = reduced_rhs.shape[1]
    npts = point_damp.shape[0]
    point_mat = point_matrix(point_jac, point_idx, npts) + point_damp[None, None, :] * jnp.eye(3, dtype=jnp.float32)[:, :, None]
    point_inv = invert3(point_mat)
    cam_diag = camera_diag_terms(cam_jac, cam_idx, ncam) + cam_damp[None, :]

    def operate(vec):
        y = jnp.einsum("rko,ko->ro", cam_jac, vec[:, cam_idx], precision=HI)
        u = segsum(jnp.einsum("rao,ro->ao", point_jac, y, precision=HI), point_idx, npts)
        w = jnp.sum(point_inv * u[None, :, :], axis=1)
        z = y - jnp.einsum("rao,ao->ro", point_jac, w[:, point_idx], precision=HI)
        return cam_damp[None, :] * vec + segsum(jnp.einsum("rko,ro->ko", cam_jac, z, precision=HI), cam_idx, ncam)

    solution = jnp.zeros_like(reduced_rhs)
    residual = reduced_rhs
    pre = residual / cam_diag
    direction = pre
    rz = jnp.sum(residual * pre)
    for step in range(ITERS):
        image = operate(direction)
        alpha = rz / jnp.sum(direction * image)
        solution = solution + alpha * direction
        residual = residual - alpha * image
        pre = residual / cam_diag
        new_rz = jnp.sum(residual * pre)
        direction = pre + (new_rz / rz) * direction
        rz = new_rz
    return solution, residual
```

```python
import jax
import jax.numpy as jnp
from jax import lax
from jax.sharding import PartitionSpec as P

ITERS = 3

BF = jnp.bfloat16
F32 = jnp.float32


def split_of(count):
    lo = 1 << (max(count.bit_length() - 1, 0) // 2)
    while count % lo:
        lo //= 2
    return count // lo, lo


def pieces(value):
    first = lax.reduce_precision(value, exponent_bits=8, mantissa_bits=7)
    rest = value - first
    second = lax.reduce_precision(rest, exponent_bits=8, mantissa_bits=7)
    third = rest - second
    return first.astype(BF), second.astype(BF), third.astype(BF)


class Index:
    def __init__(self, index, count):
        self.count = count
        self.hi, self.lo = split_of(count)
        high = index // self.lo
        low = index % self.lo
        hot = (lax.broadcasted_iota(jnp.int32, (self.hi, index.shape[0]), 0) == high[None, :])
        self.hot = hot.astype(BF)
        self.hot3 = jnp.concatenate([self.hot] * 3, axis=1)
        self.hot3t = jnp.concatenate([self.hot] * 3, axis=0)
        self.low = lax.broadcasted_iota(jnp.int32, (self.lo, index.shape[0]), 0) == low[None, :]

    def segsum(self, terms):
        ncol = terms.shape[0]
        parts = [
            jnp.where(self.low[None], part[:, None, :], jnp.zeros((), BF)).reshape(ncol * self.lo, -1)
            for part in pieces(terms)
        ]
        spread = jnp.concatenate(parts, axis=1)
        out = lax.dot_general(
            self.hot3, spread, (((1,), (1,)), ((), ())), preferred_element_type=F32
        )
        return out.reshape(self.hi, ncol, self.lo).transpose(1, 0, 2).reshape(ncol, self.count)

    def gather(self, table):
        ncol = table.shape[0]
        mat = table.reshape(ncol, self.hi, self.lo).transpose(0, 2, 1).reshape(ncol * self.lo, self.hi)
        stacked = jnp.concatenate(pieces(mat), axis=1)
        spread = lax.dot_general(
            stacked, self.hot3t, (((1,), (0,)), ((), ())), preferred_element_type=F32
        ).reshape(ncol, self.lo, -1)
        return jnp.sum(jnp.where(self.low[None], spread, 0.0), axis=1)


def invert3(mat):
    c00 = mat[1, 1] * mat[2, 2] - mat[1, 2] * mat[2, 1]
    c01 = mat[0, 2] * mat[2, 1] - mat[0, 1] * mat[2, 2]
    c02 = mat[0, 1] * mat[1, 2] - mat[0, 2] * mat[1, 1]
    c10 = mat[1, 2] * mat[2, 0] - mat[1, 0] * mat[2, 2]
    c11 = mat[0, 0] * mat[2, 2] - mat[0, 2] * mat[2, 0]
    c12 = mat[0, 2] * mat[1, 0] - mat[0, 0] * mat[1, 2]
    c20 = mat[1, 0] * mat[2, 1] - mat[1, 1] * mat[2, 0]
    c21 = mat[0, 1] * mat[2, 0] - mat[0, 0] * mat[2, 1]
    c22 = mat[0, 0] * mat[1, 1] - mat[0, 1] * mat[1, 0]
    det = mat[0, 0] * c00 + mat[0, 1] * c10 + mat[0, 2] * c20
    adj = jnp.stack(
        [jnp.stack([c00, c01, c02]), jnp.stack([c10, c11, c12]), jnp.stack([c20, c21, c22])]
    )
    return adj / det


def normal_six(point_jac):
    pairs = [(0, 0), (0, 1), (0, 2), (1, 1), (1, 2), (2, 2)]
    return jnp.stack(
        [jnp.sum(point_jac[:, first] * point_jac[:, second], axis=0) for first, second in pairs]
    )


def expand_six(six):
    return jnp.stack(
        [
            jnp.stack([six[0], six[1], six[2]]),
            jnp.stack([six[1], six[3], six[4]]),
            jnp.stack([six[2], six[4], six[5]]),
        ]
    )


def point_inverse(six, damp):
    mat = expand_six(six) + damp[None, None, :] * jnp.eye(3, dtype=jnp.float32)[:, :, None]
    return invert3(mat)


def norm_sum(value):
    return lax.psum(value, "cam")


def on_device(cam_jac, point_jac, obs_cam, obs_point, point_damp, cam_damp, reduced_rhs):
    npts = point_damp.shape[0]
    ncam = reduced_rhs.shape[1]
    by_point = Index(obs_point, npts)
    by_cam = Index(obs_cam, ncam)
    six_terms = by_point.segsum(normal_six(point_jac))
    pshare = npts // lax.axis_size("cam")
    pstart = lax.axis_index("cam") * pshare
    six_share = lax.psum_scatter(six_terms, "cam", scatter_dimension=1, tiled=True)
    damp_pts = lax.dynamic_slice_in_dim(point_damp, pstart, pshare, 0)
    inv_share = point_inverse(six_share, damp_pts)
    diag_terms = by_cam.segsum(jnp.sum(cam_jac * cam_jac, axis=0))
    cam_diag = lax.psum(diag_terms, "pts") + cam_damp[None, :]
    solution = jnp.zeros_like(reduced_rhs)
    residual = reduced_rhs
    pre = residual / cam_diag
    direction = pre
    rz = norm_sum(jnp.sum(residual * pre))
    for step in range(ITERS):
        dir_obs = by_cam.gather(direction)
        y = jnp.sum(cam_jac * dir_obs[None], axis=1)
        reduced_u_part = by_point.segsum(jnp.sum(point_jac * y[:, None, :], axis=0))
        u_share = lax.psum_scatter(reduced_u_part, "cam", scatter_dimension=1, tiled=True)
        w_share = jnp.sum(inv_share * u_share[None, :, :], axis=1)
        w = lax.all_gather(w_share, "cam", axis=1, tiled=True)
        z = y - jnp.sum(point_jac * by_point.gather(w)[None], axis=1)
        image = cam_damp[None, :] * direction + lax.psum(
            by_cam.segsum(jnp.sum(cam_jac * z[:, None, :], axis=0)), "pts"
        )
        alpha = rz / lax.psum(jnp.sum(direction * image), "cam")
        solution = solution + alpha * direction
        residual = residual - alpha * image
        pre = residual / cam_diag
        new_rz = norm_sum(jnp.sum(residual * pre))
        direction = pre + new_rz / rz * direction
        rz = new_rz
    return (solution, residual)


def solution(mesh):
    return jax.shard_map(
        on_device,
        mesh=mesh,
        in_specs=(
            P(None, None, ("groups", "pts", "cam")),
            P(None, None, ("groups", "pts", "cam")),
            P(("groups", "pts", "cam")),
            P(("groups", "pts", "cam")),
            P(("groups", "pts")),
            P(("groups", "cam")),
            P(None, ("groups", "cam")),
        ),
        out_specs=(P(None, ("groups", "cam")), P(None, ("groups", "cam"))),
        check_vma=False,
    )
```

```python
import jax
import jax.numpy as jnp
from jax import lax
from jax.sharding import PartitionSpec as P

ITERS = 3

BF = jnp.bfloat16
F32 = jnp.float32


def split_of(count):
    lo = 1 << (max(count.bit_length() - 1, 0) // 2)
    while count % lo:
        lo //= 2
    return count // lo, lo


def pieces(value):
    first = lax.reduce_precision(value, exponent_bits=8, mantissa_bits=7)
    rest = value - first
    second = lax.reduce_precision(rest, exponent_bits=8, mantissa_bits=7)
    third = rest - second
    return first.astype(BF), second.astype(BF), third.astype(BF)


class Index:
    def __init__(self, index, count):
        self.count = count
        self.hi, self.lo = split_of(count)
        high = index // self.lo
        low = index % self.lo
        hot = (lax.broadcasted_iota(jnp.int32, (self.hi, index.shape[0]), 0) == high[None, :])
        self.hot = hot.astype(BF)
        self.hot3 = jnp.concatenate([self.hot] * 3, axis=1)
        self.hot3t = jnp.concatenate([self.hot] * 3, axis=0)
        self.low = lax.broadcasted_iota(jnp.int32, (self.lo, index.shape[0]), 0) == low[None, :]

    def segsum(self, terms):
        ncol = terms.shape[0]
        parts = [
            jnp.where(self.low[None], part[:, None, :], jnp.zeros((), BF)).reshape(ncol * self.lo, -1)
            for part in pieces(terms)
        ]
        spread = jnp.concatenate(parts, axis=1)
        out = lax.dot_general(
            self.hot3, spread, (((1,), (1,)), ((), ())), preferred_element_type=F32
        )
        return out.reshape(self.hi, ncol, self.lo).transpose(1, 0, 2).reshape(ncol, self.count)

    def gather(self, table):
        ncol = table.shape[0]
        mat = table.reshape(ncol, self.hi, self.lo).transpose(0, 2, 1).reshape(ncol * self.lo, self.hi)
        stacked = jnp.concatenate(pieces(mat), axis=1)
        spread = lax.dot_general(
            stacked, self.hot3t, (((1,), (0,)), ((), ())), preferred_element_type=F32
        ).reshape(ncol, self.lo, -1)
        return jnp.sum(jnp.where(self.low[None], spread, 0.0), axis=1)


def invert3(mat):
    c00 = mat[1, 1] * mat[2, 2] - mat[1, 2] * mat[2, 1]
    c01 = mat[0, 2] * mat[2, 1] - mat[0, 1] * mat[2, 2]
    c02 = mat[0, 1] * mat[1, 2] - mat[0, 2] * mat[1, 1]
    c10 = mat[1, 2] * mat[2, 0] - mat[1, 0] * mat[2, 2]
    c11 = mat[0, 0] * mat[2, 2] - mat[0, 2] * mat[2, 0]
    c12 = mat[0, 2] * mat[1, 0] - mat[0, 0] * mat[1, 2]
    c20 = mat[1, 0] * mat[2, 1] - mat[1, 1] * mat[2, 0]
    c21 = mat[0, 1] * mat[2, 0] - mat[0, 0] * mat[2, 1]
    c22 = mat[0, 0] * mat[1, 1] - mat[0, 1] * mat[1, 0]
    det = mat[0, 0] * c00 + mat[0, 1] * c10 + mat[0, 2] * c20
    adj = jnp.stack(
        [jnp.stack([c00, c01, c02]), jnp.stack([c10, c11, c12]), jnp.stack([c20, c21, c22])]
    )
    return adj / det


def normal_six(point_jac):
    pairs = [(0, 0), (0, 1), (0, 2), (1, 1), (1, 2), (2, 2)]
    return jnp.stack(
        [jnp.sum(point_jac[:, first] * point_jac[:, second], axis=0) for first, second in pairs]
    )


def expand_six(six):
    return jnp.stack(
        [
            jnp.stack([six[0], six[1], six[2]]),
            jnp.stack([six[1], six[3], six[4]]),
            jnp.stack([six[2], six[4], six[5]]),
        ]
    )


def point_inverse(six, damp):
    mat = expand_six(six) + damp[None, None, :] * jnp.eye(3, dtype=jnp.float32)[:, :, None]
    return invert3(mat)


SIZES = {}


def allsum(value, axis):
    size = SIZES[axis]
    if size & (size - 1):
        return lax.psum(value, axis)
    step = 1
    while step < size:
        value = value + lax.ppermute(value, axis, [(i, i ^ step) for i in range(size)])
        step *= 2
    return value


def norm_sum(value):
    return allsum(value, "cam")


def on_device(cam_jac, point_jac, obs_cam, obs_point, point_damp, cam_damp, reduced_rhs):
    npts = point_damp.shape[0]
    ncam = reduced_rhs.shape[1]
    by_point = Index(obs_point, npts)
    by_cam = Index(obs_cam, ncam)
    six_terms = allsum(by_point.segsum(normal_six(point_jac)), "cam")
    inv = point_inverse(six_terms, point_damp)
    diag_terms = by_cam.segsum(jnp.sum(cam_jac * cam_jac, axis=0))
    cam_diag = allsum(diag_terms, "pts") + cam_damp[None, :]
    solution = jnp.zeros_like(reduced_rhs)
    residual = reduced_rhs
    pre = residual / cam_diag
    direction = pre
    rz = norm_sum(jnp.sum(residual * pre))
    for step in range(ITERS):
        dir_obs = by_cam.gather(direction)
        y = jnp.sum(cam_jac * dir_obs[None], axis=1)
        u = allsum(by_point.segsum(jnp.sum(point_jac * y[:, None, :], axis=0)), "cam")
        w = jnp.sum(inv * u[None, :, :], axis=1)
        z = y - jnp.sum(point_jac * by_point.gather(w)[None], axis=1)
        image = cam_damp[None, :] * direction + allsum(
            by_cam.segsum(jnp.sum(cam_jac * z[:, None, :], axis=0)), "pts"
        )
        alpha = rz / allsum(jnp.sum(direction * image), "cam")
        solution = solution + alpha * direction
        residual = residual - alpha * image
        pre = residual / cam_diag
        new_rz = norm_sum(jnp.sum(residual * pre))
        direction = pre + new_rz / rz * direction
        rz = new_rz
    return (solution, residual)


def solution(mesh):
    SIZES.update(mesh.shape)
    return jax.shard_map(
        on_device,
        mesh=mesh,
        in_specs=(
            P(None, None, ("groups", "pts", "cam")),
            P(None, None, ("groups", "pts", "cam")),
            P(("groups", "pts", "cam")),
            P(("groups", "pts", "cam")),
            P(("groups", "pts")),
            P(("groups", "cam")),
            P(None, ("groups", "cam")),
        ),
        out_specs=(P(None, ("groups", "cam")), P(None, ("groups", "cam"))),
        check_vma=False,
    )
```

```python
import jax
import jax.numpy as jnp
from jax import lax
from jax.sharding import PartitionSpec as P

ITERS = 3

BF = jnp.bfloat16
F32 = jnp.float32


def split_of(count):
    lo = 1 << (max(count.bit_length() - 1, 0) // 2)
    while count % lo:
        lo //= 2
    return count // lo, lo


def pieces(value):
    first = lax.reduce_precision(value, exponent_bits=8, mantissa_bits=7)
    rest = value - first
    second = lax.reduce_precision(rest, exponent_bits=8, mantissa_bits=7)
    third = rest - second
    return first.astype(BF), second.astype(BF), third.astype(BF)


class Index:
    def __init__(self, index, count):
        self.count = count
        self.hi, self.lo = split_of(count)
        high = index // self.lo
        low = index % self.lo
        hot = (lax.broadcasted_iota(jnp.int32, (self.hi, index.shape[0]), 0) == high[None, :])
        self.hot = hot.astype(BF)
        self.hot3 = jnp.concatenate([self.hot] * 3, axis=1)
        self.hot3t = jnp.concatenate([self.hot] * 3, axis=0)
        self.low = lax.broadcasted_iota(jnp.int32, (self.lo, index.shape[0]), 0) == low[None, :]

    def segsum(self, terms):
        ncol = terms.shape[0]
        parts = [
            jnp.where(self.low[None], part[:, None, :], jnp.zeros((), BF)).reshape(ncol * self.lo, -1)
            for part in pieces(terms)
        ]
        spread = jnp.concatenate(parts, axis=1)
        out = lax.dot_general(
            self.hot3, spread, (((1,), (1,)), ((), ())), preferred_element_type=F32
        )
        return out.reshape(self.hi, ncol, self.lo).transpose(1, 0, 2).reshape(ncol, self.count)

    def gather(self, table):
        ncol = table.shape[0]
        mat = table.reshape(ncol, self.hi, self.lo).transpose(0, 2, 1).reshape(ncol * self.lo, self.hi)
        stacked = jnp.concatenate(pieces(mat), axis=1)
        spread = lax.dot_general(
            stacked, self.hot3t, (((1,), (0,)), ((), ())), preferred_element_type=F32
        ).reshape(ncol, self.lo, -1)
        return jnp.sum(jnp.where(self.low[None], spread, 0.0), axis=1)


def invert3(mat):
    c00 = mat[1, 1] * mat[2, 2] - mat[1, 2] * mat[2, 1]
    c01 = mat[0, 2] * mat[2, 1] - mat[0, 1] * mat[2, 2]
    c02 = mat[0, 1] * mat[1, 2] - mat[0, 2] * mat[1, 1]
    c10 = mat[1, 2] * mat[2, 0] - mat[1, 0] * mat[2, 2]
    c11 = mat[0, 0] * mat[2, 2] - mat[0, 2] * mat[2, 0]
    c12 = mat[0, 2] * mat[1, 0] - mat[0, 0] * mat[1, 2]
    c20 = mat[1, 0] * mat[2, 1] - mat[1, 1] * mat[2, 0]
    c21 = mat[0, 1] * mat[2, 0] - mat[0, 0] * mat[2, 1]
    c22 = mat[0, 0] * mat[1, 1] - mat[0, 1] * mat[1, 0]
    det = mat[0, 0] * c00 + mat[0, 1] * c10 + mat[0, 2] * c20
    adj = jnp.stack(
        [jnp.stack([c00, c01, c02]), jnp.stack([c10, c11, c12]), jnp.stack([c20, c21, c22])]
    )
    return adj / det


def normal_six(point_jac):
    pairs = [(0, 0), (0, 1), (0, 2), (1, 1), (1, 2), (2, 2)]
    return jnp.stack(
        [jnp.sum(point_jac[:, first] * point_jac[:, second], axis=0) for first, second in pairs]
    )


def expand_six(six):
    return jnp.stack(
        [
            jnp.stack([six[0], six[1], six[2]]),
            jnp.stack([six[1], six[3], six[4]]),
            jnp.stack([six[2], six[4], six[5]]),
        ]
    )


def point_inverse(six, damp):
    mat = expand_six(six) + damp[None, None, :] * jnp.eye(3, dtype=jnp.float32)[:, :, None]
    return invert3(mat)


SIZES = {}


def allsum(value, axis):
    size = SIZES[axis]
    if size <= 4:
        me = lax.axis_index(axis)
        got = [value] + [
            lax.ppermute(value, axis, [(i, (i + shift) % size) for i in range(size)])
            for shift in range(1, size)
        ]
        stacked = jnp.stack(got)
        ordered = [stacked[(me - source) % size] for source in range(size)]
        while len(ordered) > 1:
            ordered = [ordered[i] + ordered[i + 1] if i + 1 < len(ordered) else ordered[i]
                       for i in range(0, len(ordered), 2)]
        return ordered[0]
    if size & (size - 1):
        return lax.psum(value, axis)
    step = 1
    while step < size:
        value = value + lax.ppermute(value, axis, [(i, i ^ step) for i in range(size)])
        step *= 2
    return value


def norm_sum(value):
    return allsum(value, "cam")


def on_device(cam_jac, point_jac, obs_cam, obs_point, point_damp, cam_damp, reduced_rhs):
    npts = point_damp.shape[0]
    ncam = reduced_rhs.shape[1]
    by_point = Index(obs_point, npts)
    by_cam = Index(obs_cam, ncam)
    six_terms = allsum(by_point.segsum(normal_six(point_jac)), "cam")
    inv = point_inverse(six_terms, point_damp)
    diag_terms = by_cam.segsum(jnp.sum(cam_jac * cam_jac, axis=0))
    cam_diag = allsum(diag_terms, "pts") + cam_damp[None, :]
    solution = jnp.zeros_like(reduced_rhs)
    residual = reduced_rhs
    pre = residual / cam_diag
    direction = pre
    rz = norm_sum(jnp.sum(residual * pre))
    for step in range(ITERS):
        dir_obs = by_cam.gather(direction)
        y = jnp.sum(cam_jac * dir_obs[None], axis=1)
        u = allsum(by_point.segsum(jnp.sum(point_jac * y[:, None, :], axis=0)), "cam")
        w = jnp.sum(inv * u[None, :, :], axis=1)
        z = y - jnp.sum(point_jac * by_point.gather(w)[None], axis=1)
        image = cam_damp[None, :] * direction + allsum(
            by_cam.segsum(jnp.sum(cam_jac * z[:, None, :], axis=0)), "pts"
        )
        alpha = rz / allsum(jnp.sum(direction * image), "cam")
        solution = solution + alpha * direction
        residual = residual - alpha * image
        pre = residual / cam_diag
        new_rz = norm_sum(jnp.sum(residual * pre))
        direction = pre + new_rz / rz * direction
        rz = new_rz
    return (solution, residual)


def solution(mesh):
    SIZES.update(mesh.shape)
    return jax.shard_map(
        on_device,
        mesh=mesh,
        in_specs=(
            P(None, None, ("groups", "pts", "cam")),
            P(None, None, ("groups", "pts", "cam")),
            P(("groups", "pts", "cam")),
            P(("groups", "pts", "cam")),
            P(("groups", "pts")),
            P(("groups", "cam")),
            P(None, ("groups", "cam")),
        ),
        out_specs=(P(None, ("groups", "cam")), P(None, ("groups", "cam"))),
        check_vma=False,
    )
```

```python
import jax
import jax.numpy as jnp
from jax import lax
from jax.sharding import PartitionSpec as P

ITERS = 3

BF = jnp.bfloat16
F32 = jnp.float32


def split_of(count):
    lo = 1 << (max(count.bit_length() - 1, 0) // 2)
    while count % lo:
        lo //= 2
    return count // lo, lo


def pieces(value):
    first = lax.reduce_precision(value, exponent_bits=8, mantissa_bits=7)
    rest = value - first
    second = lax.reduce_precision(rest, exponent_bits=8, mantissa_bits=7)
    third = rest - second
    return first.astype(BF), second.astype(BF), third.astype(BF)


class Index:
    def __init__(self, index, count):
        self.count = count
        self.hi, self.lo = split_of(count)
        high = index // self.lo
        low = index % self.lo
        hot = (lax.broadcasted_iota(jnp.int32, (self.hi, index.shape[0]), 0) == high[None, :])
        self.hot = hot.astype(BF)
        self.hot3 = jnp.concatenate([self.hot] * 3, axis=1)
        self.hot3t = jnp.concatenate([self.hot] * 3, axis=0)
        self.low = lax.broadcasted_iota(jnp.int32, (self.lo, index.shape[0]), 0) == low[None, :]

    def segsum(self, terms):
        ncol = terms.shape[0]
        parts = [
            jnp.where(self.low[None], part[:, None, :], jnp.zeros((), BF)).reshape(ncol * self.lo, -1)
            for part in pieces(terms)
        ]
        spread = jnp.concatenate(parts, axis=1)
        out = lax.dot_general(
            self.hot3, spread, (((1,), (1,)), ((), ())), preferred_element_type=F32
        )
        return out.reshape(self.hi, ncol, self.lo).transpose(1, 0, 2).reshape(ncol, self.count)

    def gather(self, table):
        ncol = table.shape[0]
        mat = table.reshape(ncol, self.hi, self.lo).transpose(0, 2, 1).reshape(ncol * self.lo, self.hi)
        stacked = jnp.concatenate(pieces(mat), axis=1)
        spread = lax.dot_general(
            stacked, self.hot3t, (((1,), (0,)), ((), ())), preferred_element_type=F32
        ).reshape(ncol, self.lo, -1)
        return jnp.sum(jnp.where(self.low[None], spread, 0.0), axis=1)


def invert3(mat):
    c00 = mat[1, 1] * mat[2, 2] - mat[1, 2] * mat[2, 1]
    c01 = mat[0, 2] * mat[2, 1] - mat[0, 1] * mat[2, 2]
    c02 = mat[0, 1] * mat[1, 2] - mat[0, 2] * mat[1, 1]
    c10 = mat[1, 2] * mat[2, 0] - mat[1, 0] * mat[2, 2]
    c11 = mat[0, 0] * mat[2, 2] - mat[0, 2] * mat[2, 0]
    c12 = mat[0, 2] * mat[1, 0] - mat[0, 0] * mat[1, 2]
    c20 = mat[1, 0] * mat[2, 1] - mat[1, 1] * mat[2, 0]
    c21 = mat[0, 1] * mat[2, 0] - mat[0, 0] * mat[2, 1]
    c22 = mat[0, 0] * mat[1, 1] - mat[0, 1] * mat[1, 0]
    det = mat[0, 0] * c00 + mat[0, 1] * c10 + mat[0, 2] * c20
    adj = jnp.stack(
        [jnp.stack([c00, c01, c02]), jnp.stack([c10, c11, c12]), jnp.stack([c20, c21, c22])]
    )
    return adj / det


def normal_six(point_jac):
    pairs = [(0, 0), (0, 1), (0, 2), (1, 1), (1, 2), (2, 2)]
    return jnp.stack(
        [jnp.sum(point_jac[:, first] * point_jac[:, second], axis=0) for first, second in pairs]
    )


def expand_six(six):
    return jnp.stack(
        [
            jnp.stack([six[0], six[1], six[2]]),
            jnp.stack([six[1], six[3], six[4]]),
            jnp.stack([six[2], six[4], six[5]]),
        ]
    )


def point_inverse(six, damp):
    mat = expand_six(six) + damp[None, None, :] * jnp.eye(3, dtype=jnp.float32)[:, :, None]
    return invert3(mat)


SIZES = {}


def allsum(value, axis):
    size = SIZES[axis]
    if size == 4:
        peers = [
            lax.ppermute(value, axis, [(i, i ^ mask) for i in range(size)]) for mask in (1, 2, 3)
        ]
        return (value + peers[0]) + (peers[1] + peers[2])
    if size & (size - 1):
        return lax.psum(value, axis)
    step = 1
    while step < size:
        value = value + lax.ppermute(value, axis, [(i, i ^ step) for i in range(size)])
        step *= 2
    return value


def norm_sum(value):
    return allsum(value, "cam")


def on_device(cam_jac, point_jac, obs_cam, obs_point, point_damp, cam_damp, reduced_rhs):
    npts = point_damp.shape[0]
    ncam = reduced_rhs.shape[1]
    by_point = Index(obs_point, npts)
    by_cam = Index(obs_cam, ncam)
    six_terms = allsum(by_point.segsum(normal_six(point_jac)), "cam")
    inv = point_inverse(six_terms, point_damp)
    diag_terms = by_cam.segsum(jnp.sum(cam_jac * cam_jac, axis=0))
    cam_diag = allsum(diag_terms, "pts") + cam_damp[None, :]
    solution = jnp.zeros_like(reduced_rhs)
    residual = reduced_rhs
    pre = residual / cam_diag
    direction = pre
    rz = norm_sum(jnp.sum(residual * pre))
    for step in range(ITERS):
        dir_obs = by_cam.gather(direction)
        y = jnp.sum(cam_jac * dir_obs[None], axis=1)
        u = allsum(by_point.segsum(jnp.sum(point_jac * y[:, None, :], axis=0)), "cam")
        w = jnp.sum(inv * u[None, :, :], axis=1)
        z = y - jnp.sum(point_jac * by_point.gather(w)[None], axis=1)
        image = cam_damp[None, :] * direction + allsum(
            by_cam.segsum(jnp.sum(cam_jac * z[:, None, :], axis=0)), "pts"
        )
        alpha = rz / allsum(jnp.sum(direction * image), "cam")
        solution = solution + alpha * direction
        residual = residual - alpha * image
        pre = residual / cam_diag
        new_rz = norm_sum(jnp.sum(residual * pre))
        direction = pre + new_rz / rz * direction
        rz = new_rz
    return (solution, residual)


def solution(mesh):
    SIZES.update(mesh.shape)
    return jax.shard_map(
        on_device,
        mesh=mesh,
        in_specs=(
            P(None, None, ("groups", "pts", "cam")),
            P(None, None, ("groups", "pts", "cam")),
            P(("groups", "pts", "cam")),
            P(("groups", "pts", "cam")),
            P(("groups", "pts")),
            P(("groups", "cam")),
            P(None, ("groups", "cam")),
        ),
        out_specs=(P(None, ("groups", "cam")), P(None, ("groups", "cam"))),
        check_vma=False,
    )
```

```python
import jax
import jax.numpy as jnp
from jax import lax
from jax.sharding import PartitionSpec as P

ITERS = 3

BF = jnp.bfloat16
F32 = jnp.float32


def split_of(count):
    lo = 1 << (max(count.bit_length() - 1, 0) // 2)
    while count % lo:
        lo //= 2
    return count // lo, lo


def pieces(value):
    first = lax.reduce_precision(value, exponent_bits=8, mantissa_bits=7)
    rest = value - first
    second = lax.reduce_precision(rest, exponent_bits=8, mantissa_bits=7)
    third = rest - second
    return first.astype(BF), second.astype(BF), third.astype(BF)


class Index:
    def __init__(self, index, count):
        self.count = count
        self.hi, self.lo = split_of(count)
        high = index // self.lo
        low = index % self.lo
        hot = (lax.broadcasted_iota(jnp.int32, (self.hi, index.shape[0]), 0) == high[None, :])
        self.hot = hot.astype(BF)
        self.hot3 = jnp.concatenate([self.hot] * 3, axis=1)
        self.hot3t = jnp.concatenate([self.hot] * 3, axis=0)
        self.low = lax.broadcasted_iota(jnp.int32, (self.lo, index.shape[0]), 0) == low[None, :]

    def segsum(self, terms):
        ncol = terms.shape[0]
        parts = [
            jnp.where(self.low[None], part[:, None, :], jnp.zeros((), BF)).reshape(ncol * self.lo, -1)
            for part in pieces(terms)
        ]
        spread = jnp.concatenate(parts, axis=1)
        out = lax.dot_general(
            self.hot3, spread, (((1,), (1,)), ((), ())), preferred_element_type=F32
        )
        return out.reshape(self.hi, ncol, self.lo).transpose(1, 0, 2).reshape(ncol, self.count)

    def gather(self, table):
        ncol = table.shape[0]
        mat = table.reshape(ncol, self.hi, self.lo).transpose(0, 2, 1).reshape(ncol * self.lo, self.hi)
        stacked = jnp.concatenate(pieces(mat), axis=1)
        spread = lax.dot_general(
            stacked, self.hot3t, (((1,), (0,)), ((), ())), preferred_element_type=F32
        ).reshape(ncol, self.lo, -1)
        return jnp.sum(jnp.where(self.low[None], spread, 0.0), axis=1)


def invert3(mat):
    c00 = mat[1, 1] * mat[2, 2] - mat[1, 2] * mat[2, 1]
    c01 = mat[0, 2] * mat[2, 1] - mat[0, 1] * mat[2, 2]
    c02 = mat[0, 1] * mat[1, 2] - mat[0, 2] * mat[1, 1]
    c10 = mat[1, 2] * mat[2, 0] - mat[1, 0] * mat[2, 2]
    c11 = mat[0, 0] * mat[2, 2] - mat[0, 2] * mat[2, 0]
    c12 = mat[0, 2] * mat[1, 0] - mat[0, 0] * mat[1, 2]
    c20 = mat[1, 0] * mat[2, 1] - mat[1, 1] * mat[2, 0]
    c21 = mat[0, 1] * mat[2, 0] - mat[0, 0] * mat[2, 1]
    c22 = mat[0, 0] * mat[1, 1] - mat[0, 1] * mat[1, 0]
    det = mat[0, 0] * c00 + mat[0, 1] * c10 + mat[0, 2] * c20
    adj = jnp.stack(
        [jnp.stack([c00, c01, c02]), jnp.stack([c10, c11, c12]), jnp.stack([c20, c21, c22])]
    )
    return adj / det


def normal_six(point_jac):
    pairs = [(0, 0), (0, 1), (0, 2), (1, 1), (1, 2), (2, 2)]
    return jnp.stack(
        [jnp.sum(point_jac[:, first] * point_jac[:, second], axis=0) for first, second in pairs]
    )


def expand_six(six):
    return jnp.stack(
        [
            jnp.stack([six[0], six[1], six[2]]),
            jnp.stack([six[1], six[3], six[4]]),
            jnp.stack([six[2], six[4], six[5]]),
        ]
    )


def point_inverse(six, damp):
    mat = expand_six(six) + damp[None, None, :] * jnp.eye(3, dtype=jnp.float32)[:, :, None]
    return invert3(mat)


SIZES = {}


def allsum(value, axis):
    size = SIZES[axis]
    if size == 4:
        peers = [
            lax.ppermute(value, axis, [(i, i ^ mask) for i in range(size)]) for mask in (1, 2, 3)
        ]
        return (value + peers[0]) + (peers[1] + peers[2])
    if size & (size - 1):
        return lax.psum(value, axis)
    step = 1
    while step < size:
        value = value + lax.ppermute(value, axis, [(i, i ^ step) for i in range(size)])
        step *= 2
    return value


def norm_sum(value):
    return allsum(value, "cam")


def on_device(cam_jac, point_jac, obs_cam, obs_point, point_damp, cam_damp, reduced_rhs):
    npts = point_damp.shape[0]
    ncam = reduced_rhs.shape[1]
    by_point = Index(obs_point, npts)
    by_cam = Index(obs_cam, ncam)
    six_terms = allsum(by_point.segsum(normal_six(point_jac)), "cam")
    inv = point_inverse(six_terms, point_damp)
    diag_terms = by_cam.segsum(jnp.sum(cam_jac * cam_jac, axis=0))
    cam_diag = allsum(diag_terms, "pts") + cam_damp[None, :]

    def operate(vec):
        y = jnp.sum(cam_jac * by_cam.gather(vec)[None], axis=1)
        u = allsum(by_point.segsum(jnp.sum(point_jac * y[:, None, :], axis=0)), "cam")
        w = jnp.sum(inv * u[None, :, :], axis=1)
        z = y - jnp.sum(point_jac * by_point.gather(w)[None], axis=1)
        return cam_damp[None, :] * vec + allsum(
            by_cam.segsum(jnp.sum(cam_jac * z[:, None, :], axis=0)), "pts"
        )

    solution = jnp.zeros_like(reduced_rhs)
    residual = reduced_rhs
    pre = residual / cam_diag
    direction = pre
    image = operate(direction)
    sums = norm_sum(jnp.stack([jnp.sum(residual * pre), jnp.sum(direction * image)]))
    rz = sums[0]
    alpha = rz / sums[1]
    solution = solution + alpha * direction
    residual = residual - alpha * image
    for step in range(1, ITERS):
        pre = residual / cam_diag
        new_rz = norm_sum(jnp.sum(residual * pre))
        image_pre = operate(pre)
        beta = new_rz / rz
        direction = pre + beta * direction
        image = image_pre + beta * image
        alpha = new_rz / norm_sum(jnp.sum(direction * image))
        rz = new_rz
        solution = solution + alpha * direction
        residual = residual - alpha * image
    return (solution, residual)


def solution(mesh):
    SIZES.update(mesh.shape)
    return jax.shard_map(
        on_device,
        mesh=mesh,
        in_specs=(
            P(None, None, ("groups", "pts", "cam")),
            P(None, None, ("groups", "pts", "cam")),
            P(("groups", "pts", "cam")),
            P(("groups", "pts", "cam")),
            P(("groups", "pts")),
            P(("groups", "cam")),
            P(None, ("groups", "cam")),
        ),
        out_specs=(P(None, ("groups", "cam")), P(None, ("groups", "cam"))),
        check_vma=False,
    )
```

```python
import jax
import jax.numpy as jnp
from jax import lax
from jax.sharding import PartitionSpec as P

ITERS = 3

BF = jnp.bfloat16
F32 = jnp.float32


def split_of(count):
    lo = 1 << (max(count.bit_length() - 1, 0) // 2)
    while count % lo:
        lo //= 2
    return count // lo, lo


def pieces(value):
    first = lax.reduce_precision(value, exponent_bits=8, mantissa_bits=7)
    rest = value - first
    second = lax.reduce_precision(rest, exponent_bits=8, mantissa_bits=7)
    third = rest - second
    return first.astype(BF), second.astype(BF), third.astype(BF)


class Index:
    def __init__(self, index, count):
        self.count = count
        self.hi, self.lo = split_of(count)
        high = index // self.lo
        low = index % self.lo
        hot = (lax.broadcasted_iota(jnp.int32, (self.hi, index.shape[0]), 0) == high[None, :])
        self.hot = hot.astype(BF)
        self.hot3 = jnp.concatenate([self.hot] * 3, axis=1)
        self.hot3t = jnp.concatenate([self.hot] * 3, axis=0)
        self.low = lax.broadcasted_iota(jnp.int32, (self.lo, index.shape[0]), 0) == low[None, :]

    def segsum(self, terms):
        ncol = terms.shape[0]
        parts = [
            jnp.where(self.low[None], part[:, None, :], jnp.zeros((), BF)).reshape(ncol * self.lo, -1)
            for part in pieces(terms)
        ]
        spread = jnp.concatenate(parts, axis=1)
        out = lax.dot_general(
            self.hot3, spread, (((1,), (1,)), ((), ())), preferred_element_type=F32
        )
        return out.reshape(self.hi, ncol, self.lo).transpose(1, 0, 2).reshape(ncol, self.count)

    def gather(self, table):
        ncol = table.shape[0]
        mat = table.reshape(ncol, self.hi, self.lo).transpose(0, 2, 1).reshape(ncol * self.lo, self.hi)
        stacked = jnp.concatenate(pieces(mat), axis=1)
        spread = lax.dot_general(
            stacked, self.hot3t, (((1,), (0,)), ((), ())), preferred_element_type=F32
        ).reshape(ncol, self.lo, -1)
        return jnp.sum(jnp.where(self.low[None], spread, 0.0), axis=1)


def invert3(mat):
    c00 = mat[1, 1] * mat[2, 2] - mat[1, 2] * mat[2, 1]
    c01 = mat[0, 2] * mat[2, 1] - mat[0, 1] * mat[2, 2]
    c02 = mat[0, 1] * mat[1, 2] - mat[0, 2] * mat[1, 1]
    c10 = mat[1, 2] * mat[2, 0] - mat[1, 0] * mat[2, 2]
    c11 = mat[0, 0] * mat[2, 2] - mat[0, 2] * mat[2, 0]
    c12 = mat[0, 2] * mat[1, 0] - mat[0, 0] * mat[1, 2]
    c20 = mat[1, 0] * mat[2, 1] - mat[1, 1] * mat[2, 0]
    c21 = mat[0, 1] * mat[2, 0] - mat[0, 0] * mat[2, 1]
    c22 = mat[0, 0] * mat[1, 1] - mat[0, 1] * mat[1, 0]
    det = mat[0, 0] * c00 + mat[0, 1] * c10 + mat[0, 2] * c20
    adj = jnp.stack(
        [jnp.stack([c00, c01, c02]), jnp.stack([c10, c11, c12]), jnp.stack([c20, c21, c22])]
    )
    return adj / det


def normal_six(point_jac):
    pairs = [(0, 0), (0, 1), (0, 2), (1, 1), (1, 2), (2, 2)]
    return jnp.stack(
        [jnp.sum(point_jac[:, first] * point_jac[:, second], axis=0) for first, second in pairs]
    )


def expand_six(six):
    return jnp.stack(
        [
            jnp.stack([six[0], six[1], six[2]]),
            jnp.stack([six[1], six[3], six[4]]),
            jnp.stack([six[2], six[4], six[5]]),
        ]
    )


def point_inverse(six, damp):
    mat = expand_six(six) + damp[None, None, :] * jnp.eye(3, dtype=jnp.float32)[:, :, None]
    return invert3(mat)


SIZES = {}


def allsum(value, axis):
    size = SIZES[axis]
    if size == 4 and axis == "cam":
        peers = [
            lax.ppermute(value, axis, [(i, i ^ mask) for i in range(size)]) for mask in (1, 2, 3)
        ]
        return (value + peers[0]) + (peers[1] + peers[2])
    if size & (size - 1):
        return lax.psum(value, axis)
    step = 1
    while step < size:
        value = value + lax.ppermute(value, axis, [(i, i ^ step) for i in range(size)])
        step *= 2
    return value


def norm_sum(value):
    return allsum(value, "cam")


def on_device(cam_jac, point_jac, obs_cam, obs_point, point_damp, cam_damp, reduced_rhs):
    npts = point_damp.shape[0]
    ncam = reduced_rhs.shape[1]
    by_point = Index(obs_point, npts)
    by_cam = Index(obs_cam, ncam)
    six_terms = allsum(by_point.segsum(normal_six(point_jac)), "cam")
    inv = point_inverse(six_terms, point_damp)
    diag_terms = by_cam.segsum(jnp.sum(cam_jac * cam_jac, axis=0))
    cam_diag = allsum(diag_terms, "pts") + cam_damp[None, :]

    def operate(vec, extra):
        y = jnp.sum(cam_jac * by_cam.gather(vec)[None], axis=1)
        u_part = by_point.segsum(jnp.sum(point_jac * y[:, None, :], axis=0))
        extra_row = jnp.zeros((1, npts), F32).at[0, 0].set(extra)
        u_all = allsum(jnp.concatenate([u_part, extra_row], axis=0), "cam")
        u = u_all[:3]
        w = jnp.sum(inv * u[None, :, :], axis=1)
        z = y - jnp.sum(point_jac * by_point.gather(w)[None], axis=1)
        image = cam_damp[None, :] * vec + allsum(
            by_cam.segsum(jnp.sum(cam_jac * z[:, None, :], axis=0)), "pts"
        )
        return image, u_all[3, 0]

    solution = jnp.zeros_like(reduced_rhs)
    residual = reduced_rhs
    pre = residual / cam_diag
    direction = pre
    image, rz = operate(direction, jnp.sum(residual * pre))
    alpha = rz / norm_sum(jnp.sum(direction * image))
    solution = solution + alpha * direction
    residual = residual - alpha * image
    for step in range(1, ITERS):
        pre = residual / cam_diag
        image_pre, new_rz = operate(pre, jnp.sum(residual * pre))
        beta = new_rz / rz
        direction = pre + beta * direction
        image = image_pre + beta * image
        alpha = new_rz / norm_sum(jnp.sum(direction * image))
        rz = new_rz
        solution = solution + alpha * direction
        residual = residual - alpha * image
    return (solution, residual)


def solution(mesh):
    SIZES.update(mesh.shape)
    return jax.shard_map(
        on_device,
        mesh=mesh,
        in_specs=(
            P(None, None, ("groups", "pts", "cam")),
            P(None, None, ("groups", "pts", "cam")),
            P(("groups", "pts", "cam")),
            P(("groups", "pts", "cam")),
            P(("groups", "pts")),
            P(("groups", "cam")),
            P(None, ("groups", "cam")),
        ),
        out_specs=(P(None, ("groups", "cam")), P(None, ("groups", "cam"))),
        check_vma=False,
    )
```

```python
import jax
import jax.numpy as jnp
from jax import lax
from jax.sharding import PartitionSpec as P

ITERS = 3

BF = jnp.bfloat16
F32 = jnp.float32


def split_of(count):
    lo = 1 << (max(count.bit_length() - 1, 0) // 2)
    while count % lo:
        lo //= 2
    return count // lo, lo


def pieces(value):
    first = lax.reduce_precision(value, exponent_bits=8, mantissa_bits=7)
    rest = value - first
    second = lax.reduce_precision(rest, exponent_bits=8, mantissa_bits=7)
    third = rest - second
    return first.astype(BF), second.astype(BF), third.astype(BF)


class Index:
    def __init__(self, index, count):
        self.count = count
        self.hi, self.lo = split_of(count)
        high = index // self.lo
        low = index % self.lo
        hot = (lax.broadcasted_iota(jnp.int32, (self.hi, index.shape[0]), 0) == high[None, :])
        self.hot = hot.astype(BF)
        self.hot3 = jnp.concatenate([self.hot] * 3, axis=1)
        self.hot3t = jnp.concatenate([self.hot] * 3, axis=0)
        self.low = lax.broadcasted_iota(jnp.int32, (self.lo, index.shape[0]), 0) == low[None, :]

    def segsum(self, terms):
        ncol = terms.shape[0]
        parts = [
            jnp.where(self.low[None], part[:, None, :], jnp.zeros((), BF)).reshape(ncol * self.lo, -1)
            for part in pieces(terms)
        ]
        spread = jnp.concatenate(parts, axis=1)
        out = lax.dot_general(
            self.hot3, spread, (((1,), (1,)), ((), ())), preferred_element_type=F32
        )
        return out.reshape(self.hi, ncol, self.lo).transpose(1, 0, 2).reshape(ncol, self.count)

    def gather(self, table):
        ncol = table.shape[0]
        mat = table.reshape(ncol, self.hi, self.lo).transpose(0, 2, 1).reshape(ncol * self.lo, self.hi)
        stacked = jnp.concatenate(pieces(mat), axis=1)
        spread = lax.dot_general(
            stacked, self.hot3t, (((1,), (0,)), ((), ())), preferred_element_type=F32
        ).reshape(ncol, self.lo, -1)
        return jnp.sum(jnp.where(self.low[None], spread, 0.0), axis=1)


def invert3(mat):
    c00 = mat[1, 1] * mat[2, 2] - mat[1, 2] * mat[2, 1]
    c01 = mat[0, 2] * mat[2, 1] - mat[0, 1] * mat[2, 2]
    c02 = mat[0, 1] * mat[1, 2] - mat[0, 2] * mat[1, 1]
    c10 = mat[1, 2] * mat[2, 0] - mat[1, 0] * mat[2, 2]
    c11 = mat[0, 0] * mat[2, 2] - mat[0, 2] * mat[2, 0]
    c12 = mat[0, 2] * mat[1, 0] - mat[0, 0] * mat[1, 2]
    c20 = mat[1, 0] * mat[2, 1] - mat[1, 1] * mat[2, 0]
    c21 = mat[0, 1] * mat[2, 0] - mat[0, 0] * mat[2, 1]
    c22 = mat[0, 0] * mat[1, 1] - mat[0, 1] * mat[1, 0]
    det = mat[0, 0] * c00 + mat[0, 1] * c10 + mat[0, 2] * c20
    adj = jnp.stack(
        [jnp.stack([c00, c01, c02]), jnp.stack([c10, c11, c12]), jnp.stack([c20, c21, c22])]
    )
    return adj / det


def normal_six(point_jac):
    pairs = [(0, 0), (0, 1), (0, 2), (1, 1), (1, 2), (2, 2)]
    return jnp.stack(
        [jnp.sum(point_jac[:, first] * point_jac[:, second], axis=0) for first, second in pairs]
    )


def expand_six(six):
    return jnp.stack(
        [
            jnp.stack([six[0], six[1], six[2]]),
            jnp.stack([six[1], six[3], six[4]]),
            jnp.stack([six[2], six[4], six[5]]),
        ]
    )


def point_inverse(six, damp):
    mat = expand_six(six) + damp[None, None, :] * jnp.eye(3, dtype=jnp.float32)[:, :, None]
    return invert3(mat)


SIZES = {}


def allsum(value, axis):
    size = SIZES[axis]
    if size == 4 and axis == "cam":
        peers = [
            lax.ppermute(value, axis, [(i, i ^ mask) for i in range(size)]) for mask in (1, 2, 3)
        ]
        return (value + peers[0]) + (peers[1] + peers[2])
    if size & (size - 1):
        return lax.psum(value, axis)
    step = 1
    while step < size:
        value = value + lax.ppermute(value, axis, [(i, i ^ step) for i in range(size)])
        step *= 2
    return value


def norm_sum(value):
    return allsum(value, "cam")


def on_device(cam_jac, point_jac, obs_cam, obs_point, point_damp, cam_damp, reduced_rhs):
    npts = point_damp.shape[0]
    ncam = reduced_rhs.shape[1]
    by_point = Index(obs_point, npts)
    by_cam = Index(obs_cam, ncam)
    six_terms = allsum(by_point.segsum(normal_six(point_jac)), "cam")
    inv = point_inverse(six_terms, point_damp)
    diag_terms = by_cam.segsum(jnp.sum(cam_jac * cam_jac, axis=0))
    cam_diag = allsum(diag_terms, "pts") + cam_damp[None, :]

    def operate(vec, extras):
        y = jnp.sum(cam_jac * by_cam.gather(vec)[None], axis=1)
        u_part = by_point.segsum(jnp.sum(point_jac * y[:, None, :], axis=0))
        extras = extras + [jnp.sum(cam_damp[None, :] * vec * vec), jnp.sum(y * y)]
        count = len(extras)
        extra_row = jnp.zeros((1, npts), F32).at[0, :count].set(jnp.stack(extras))
        u_all = allsum(jnp.concatenate([u_part, extra_row], axis=0), "cam")
        u = u_all[:3]
        got = u_all[3, :count]
        w = jnp.sum(inv * u[None, :, :], axis=1)
        point_energy = got[count - 1] - jnp.sum(u * w)
        z = y - jnp.sum(point_jac * by_point.gather(w)[None], axis=1)
        img_part = by_cam.segsum(jnp.sum(cam_jac * z[:, None, :], axis=0))
        pt_row = jnp.zeros((1, ncam), F32).at[0, 0].set(point_energy)
        img_all = allsum(jnp.concatenate([img_part, pt_row], axis=0), "pts")
        image = cam_damp[None, :] * vec + img_all[:-1]
        energy = got[count - 2] + img_all[-1, 0]
        return image, got, energy

    solution = jnp.zeros_like(reduced_rhs)
    residual = reduced_rhs
    pre = residual / cam_diag
    direction = pre
    image, got, curv = operate(direction, [jnp.sum(residual * pre)])
    rz = got[0]
    alpha = rz / curv
    solution = solution + alpha * direction
    residual = residual - alpha * image
    for step in range(1, ITERS):
        pre = residual / cam_diag
        image_pre, got, energy = operate(pre, [jnp.sum(residual * pre), jnp.sum(pre * image)])
        new_rz = got[0]
        beta = new_rz / rz
        direction = pre + beta * direction
        image = image_pre + beta * image
        curv = energy + beta * (2.0 * got[1] + beta * curv)
        alpha = new_rz / curv
        rz = new_rz
        solution = solution + alpha * direction
        residual = residual - alpha * image
    return (solution, residual)


def solution(mesh):
    SIZES.update(mesh.shape)
    return jax.shard_map(
        on_device,
        mesh=mesh,
        in_specs=(
            P(None, None, ("groups", "pts", "cam")),
            P(None, None, ("groups", "pts", "cam")),
            P(("groups", "pts", "cam")),
            P(("groups", "pts", "cam")),
            P(("groups", "pts")),
            P(("groups", "cam")),
            P(None, ("groups", "cam")),
        ),
        out_specs=(P(None, ("groups", "cam")), P(None, ("groups", "cam"))),
        check_vma=False,
    )
```

```python
import jax
import jax.numpy as jnp
from jax import lax
from jax.sharding import PartitionSpec as P

ITERS = 3

BF = jnp.bfloat16
F32 = jnp.float32


def split_of(count):
    lo = 1 << (max(count.bit_length() - 1, 0) // 2)
    while count % lo:
        lo //= 2
    return count // lo, lo


def pieces(value):
    first = lax.reduce_precision(value, exponent_bits=8, mantissa_bits=7)
    rest = value - first
    second = lax.reduce_precision(rest, exponent_bits=8, mantissa_bits=7)
    third = rest - second
    return first.astype(BF), second.astype(BF), third.astype(BF)


class Index:
    def __init__(self, index, count):
        self.count = count
        self.hi, self.lo = split_of(count)
        high = index // self.lo
        low = index % self.lo
        hot = (lax.broadcasted_iota(jnp.int32, (self.hi, index.shape[0]), 0) == high[None, :])
        self.hot = hot.astype(BF)
        self.hot3 = jnp.concatenate([self.hot] * 3, axis=1)
        self.hot3t = jnp.concatenate([self.hot] * 3, axis=0)
        self.low = lax.broadcasted_iota(jnp.int32, (self.lo, index.shape[0]), 0) == low[None, :]

    def segsum(self, terms):
        ncol = terms.shape[0]
        parts = [
            jnp.where(self.low[None], part[:, None, :], jnp.zeros((), BF)).reshape(ncol * self.lo, -1)
            for part in pieces(terms)
        ]
        spread = jnp.concatenate(parts, axis=1)
        out = lax.dot_general(
            self.hot3, spread, (((1,), (1,)), ((), ())), preferred_element_type=F32
        )
        return out.reshape(self.hi, ncol, self.lo).transpose(1, 0, 2).reshape(ncol, self.count)

    def gather(self, table):
        ncol = table.shape[0]
        mat = table.reshape(ncol, self.hi, self.lo).transpose(0, 2, 1).reshape(ncol * self.lo, self.hi)
        stacked = jnp.concatenate(pieces(mat), axis=1)
        spread = lax.dot_general(
            stacked, self.hot3t, (((1,), (0,)), ((), ())), preferred_element_type=F32
        ).reshape(ncol, self.lo, -1)
        return jnp.sum(jnp.where(self.low[None], spread, 0.0), axis=1)


def invert3(mat):
    c00 = mat[1, 1] * mat[2, 2] - mat[1, 2] * mat[2, 1]
    c01 = mat[0, 2] * mat[2, 1] - mat[0, 1] * mat[2, 2]
    c02 = mat[0, 1] * mat[1, 2] - mat[0, 2] * mat[1, 1]
    c10 = mat[1, 2] * mat[2, 0] - mat[1, 0] * mat[2, 2]
    c11 = mat[0, 0] * mat[2, 2] - mat[0, 2] * mat[2, 0]
    c12 = mat[0, 2] * mat[1, 0] - mat[0, 0] * mat[1, 2]
    c20 = mat[1, 0] * mat[2, 1] - mat[1, 1] * mat[2, 0]
    c21 = mat[0, 1] * mat[2, 0] - mat[0, 0] * mat[2, 1]
    c22 = mat[0, 0] * mat[1, 1] - mat[0, 1] * mat[1, 0]
    det = mat[0, 0] * c00 + mat[0, 1] * c10 + mat[0, 2] * c20
    adj = jnp.stack(
        [jnp.stack([c00, c01, c02]), jnp.stack([c10, c11, c12]), jnp.stack([c20, c21, c22])]
    )
    return adj / det


def normal_six(point_jac):
    pairs = [(0, 0), (0, 1), (0, 2), (1, 1), (1, 2), (2, 2)]
    return jnp.stack(
        [jnp.sum(point_jac[:, first] * point_jac[:, second], axis=0) for first, second in pairs]
    )


def expand_six(six):
    return jnp.stack(
        [
            jnp.stack([six[0], six[1], six[2]]),
            jnp.stack([six[1], six[3], six[4]]),
            jnp.stack([six[2], six[4], six[5]]),
        ]
    )


def point_inverse(six, damp):
    mat = expand_six(six) + damp[None, None, :] * jnp.eye(3, dtype=jnp.float32)[:, :, None]
    return invert3(mat)


SIZES = {}


def add(first, second):
    return jax.tree.map(jnp.add, first, second)


def allsum(value, axis):
    size = SIZES[axis]
    if size == 4 and axis == "cam":
        peers = [
            lax.ppermute(value, axis, [(i, i ^ mask) for i in range(size)]) for mask in (1, 2, 3)
        ]
        return add(add(value, peers[0]), add(peers[1], peers[2]))
    if size & (size - 1):
        return lax.psum(value, axis)
    step = 1
    while step < size:
        value = add(value, lax.ppermute(value, axis, [(i, i ^ step) for i in range(size)]))
        step *= 2
    return value


def norm_sum(value):
    return allsum(value, "cam")


def on_device(cam_jac, point_jac, obs_cam, obs_point, point_damp, cam_damp, reduced_rhs):
    npts = point_damp.shape[0]
    ncam = reduced_rhs.shape[1]
    by_point = Index(obs_point, npts)
    by_cam = Index(obs_cam, ncam)
    six_terms = allsum(by_point.segsum(normal_six(point_jac)), "cam")
    inv = point_inverse(six_terms, point_damp)
    diag_terms = by_cam.segsum(jnp.sum(cam_jac * cam_jac, axis=0))
    cam_diag = allsum(diag_terms, "pts") + cam_damp[None, :]

    def operate(vec, extras):
        y = jnp.sum(cam_jac * by_cam.gather(vec)[None], axis=1)
        u_part = by_point.segsum(jnp.sum(point_jac * y[:, None, :], axis=0))
        extras = extras + [jnp.sum(cam_damp[None, :] * vec * vec), jnp.sum(y * y)]
        count = len(extras)
        u, got = allsum((u_part, jnp.stack(extras)), "cam")
        w = jnp.sum(inv * u[None, :, :], axis=1)
        point_energy = got[count - 1] - jnp.sum(u * w)
        z = y - jnp.sum(point_jac * by_point.gather(w)[None], axis=1)
        img_part = by_cam.segsum(jnp.sum(cam_jac * z[:, None, :], axis=0))
        img_sum, pt_sum = allsum((img_part, point_energy), "pts")
        image = cam_damp[None, :] * vec + img_sum
        energy = got[count - 2] + pt_sum
        return image, got, energy

    solution = jnp.zeros_like(reduced_rhs)
    residual = reduced_rhs
    pre = residual / cam_diag
    direction = pre
    image, got, curv = operate(direction, [jnp.sum(residual * pre)])
    rz = got[0]
    alpha = rz / curv
    solution = solution + alpha * direction
    residual = residual - alpha * image
    for step in range(1, ITERS):
        pre = residual / cam_diag
        image_pre, got, energy = operate(pre, [jnp.sum(residual * pre), jnp.sum(pre * image)])
        new_rz = got[0]
        beta = new_rz / rz
        direction = pre + beta * direction
        image = image_pre + beta * image
        curv = energy + beta * (2.0 * got[1] + beta * curv)
        alpha = new_rz / curv
        rz = new_rz
        solution = solution + alpha * direction
        residual = residual - alpha * image
    return (solution, residual)


def solution(mesh):
    SIZES.update(mesh.shape)
    return jax.shard_map(
        on_device,
        mesh=mesh,
        in_specs=(
            P(None, None, ("groups", "pts", "cam")),
            P(None, None, ("groups", "pts", "cam")),
            P(("groups", "pts", "cam")),
            P(("groups", "pts", "cam")),
            P(("groups", "pts")),
            P(("groups", "cam")),
            P(None, ("groups", "cam")),
        ),
        out_specs=(P(None, ("groups", "cam")), P(None, ("groups", "cam"))),
        check_vma=False,
    )
```

```python
import jax
import jax.numpy as jnp
from jax import lax
from jax.sharding import PartitionSpec as P

ITERS = 3

BF = jnp.bfloat16
F32 = jnp.float32


def split_of(count):
    lo = 1 << (max(count.bit_length() - 1, 0) // 2)
    while count % lo:
        lo //= 2
    return count // lo, lo


def pieces(value):
    first = lax.reduce_precision(value, exponent_bits=8, mantissa_bits=7)
    rest = value - first
    second = lax.reduce_precision(rest, exponent_bits=8, mantissa_bits=7)
    third = rest - second
    return first.astype(BF), second.astype(BF), third.astype(BF)


class Index:
    def __init__(self, index, count):
        self.count = count
        self.hi, self.lo = split_of(count)
        high = index // self.lo
        low = index % self.lo
        hot = (lax.broadcasted_iota(jnp.int32, (self.hi, index.shape[0]), 0) == high[None, :])
        self.hot = hot.astype(BF)
        self.hot3 = jnp.concatenate([self.hot] * 3, axis=1)
        self.hot3t = jnp.concatenate([self.hot] * 3, axis=0)
        self.low = lax.broadcasted_iota(jnp.int32, (self.lo, index.shape[0]), 0) == low[None, :]

    def segsum(self, terms):
        ncol = terms.shape[0]
        parts = [
            jnp.where(self.low[None], part[:, None, :], jnp.zeros((), BF)).reshape(ncol * self.lo, -1)
            for part in pieces(terms)
        ]
        spread = jnp.concatenate(parts, axis=1)
        out = lax.dot_general(
            self.hot3, spread, (((1,), (1,)), ((), ())), preferred_element_type=F32
        )
        return out.reshape(self.hi, ncol, self.lo).transpose(1, 0, 2).reshape(ncol, self.count)

    def gather(self, table):
        ncol = table.shape[0]
        mat = table.reshape(ncol, self.hi, self.lo).transpose(0, 2, 1).reshape(ncol * self.lo, self.hi)
        stacked = jnp.concatenate(pieces(mat), axis=1)
        spread = lax.dot_general(
            stacked, self.hot3t, (((1,), (0,)), ((), ())), preferred_element_type=F32
        ).reshape(ncol, self.lo, -1)
        return jnp.sum(jnp.where(self.low[None], spread, 0.0), axis=1)


def invert3(mat):
    c00 = mat[1, 1] * mat[2, 2] - mat[1, 2] * mat[2, 1]
    c01 = mat[0, 2] * mat[2, 1] - mat[0, 1] * mat[2, 2]
    c02 = mat[0, 1] * mat[1, 2] - mat[0, 2] * mat[1, 1]
    c10 = mat[1, 2] * mat[2, 0] - mat[1, 0] * mat[2, 2]
    c11 = mat[0, 0] * mat[2, 2] - mat[0, 2] * mat[2, 0]
    c12 = mat[0, 2] * mat[1, 0] - mat[0, 0] * mat[1, 2]
    c20 = mat[1, 0] * mat[2, 1] - mat[1, 1] * mat[2, 0]
    c21 = mat[0, 1] * mat[2, 0] - mat[0, 0] * mat[2, 1]
    c22 = mat[0, 0] * mat[1, 1] - mat[0, 1] * mat[1, 0]
    det = mat[0, 0] * c00 + mat[0, 1] * c10 + mat[0, 2] * c20
    adj = jnp.stack(
        [jnp.stack([c00, c01, c02]), jnp.stack([c10, c11, c12]), jnp.stack([c20, c21, c22])]
    )
    return adj / det


def normal_six(point_jac):
    pairs = [(0, 0), (0, 1), (0, 2), (1, 1), (1, 2), (2, 2)]
    return jnp.stack(
        [jnp.sum(point_jac[:, first] * point_jac[:, second], axis=0) for first, second in pairs]
    )


def expand_six(six):
    return jnp.stack(
        [
            jnp.stack([six[0], six[1], six[2]]),
            jnp.stack([six[1], six[3], six[4]]),
            jnp.stack([six[2], six[4], six[5]]),
        ]
    )


def point_inverse(six, damp):
    mat = expand_six(six) + damp[None, None, :] * jnp.eye(3, dtype=jnp.float32)[:, :, None]
    return invert3(mat)


SIZES = {}


def allsum(value, axis):
    size = SIZES[axis]
    if size == 4 and axis == "cam":
        peers = [
            lax.ppermute(value, axis, [(i, i ^ mask) for i in range(size)]) for mask in (1, 2, 3)
        ]
        return (value + peers[0]) + (peers[1] + peers[2])
    if size & (size - 1):
        return lax.psum(value, axis)
    step = 1
    while step < size:
        value = value + lax.ppermute(value, axis, [(i, i ^ step) for i in range(size)])
        step *= 2
    return value


def norm_sum(value):
    return allsum(value, "cam")


def on_device(cam_jac, point_jac, obs_cam, obs_point, point_damp, cam_damp, reduced_rhs):
    npts = point_damp.shape[0]
    ncam = reduced_rhs.shape[1]
    by_point = Index(obs_point, npts)
    by_cam = Index(obs_cam, ncam)
    six_terms = allsum(by_point.segsum(normal_six(point_jac)), "cam")
    inv = point_inverse(six_terms, point_damp)
    diag_terms = by_cam.segsum(jnp.sum(cam_jac * cam_jac, axis=0))
    cam_diag = allsum(diag_terms, "pts") + cam_damp[None, :]

    def as_row(rows, width):
        flat = rows.reshape(-1)
        count = -(-flat.shape[0] // width)
        return jnp.pad(flat, (0, count * width - flat.shape[0])).reshape(count, width)

    def lanes(terms):
        return jnp.sum(terms.reshape(-1, ncam), axis=0)

    def operate(vec, extras):
        y = jnp.sum(cam_jac * by_cam.gather(vec)[None], axis=1)
        u_part = by_point.segsum(jnp.sum(point_jac * y[:, None, :], axis=0))
        extras = jnp.stack([lanes(t) for t in extras] + [lanes(cam_damp[None, :] * vec * vec), lanes(y * y)])
        count = extras.shape[0]
        rows = as_row(extras, npts)
        u_all = allsum(jnp.concatenate([u_part, rows], axis=0), "cam")
        u = u_all[:3]
        got = jnp.sum(u_all[3:].reshape(-1)[: count * ncam].reshape(count, ncam), axis=1)
        w = jnp.sum(inv * u[None, :, :], axis=1)
        pt_terms = jnp.sum(u * w, axis=0).reshape(-1, ncam)
        pt_row = u_all[3:].reshape(-1)[(count - 1) * ncam : count * ncam] - jnp.sum(pt_terms, axis=0)
        z = y - jnp.sum(point_jac * by_point.gather(w)[None], axis=1)
        img_part = by_cam.segsum(jnp.sum(cam_jac * z[:, None, :], axis=0))
        img_all = allsum(jnp.concatenate([img_part, pt_row[None]], axis=0), "pts")
        image = cam_damp[None, :] * vec + img_all[:-1]
        energy = got[count - 2] + jnp.sum(img_all[-1])
        return image, got, energy

    solution = jnp.zeros_like(reduced_rhs)
    residual = reduced_rhs
    pre = residual / cam_diag
    direction = pre
    image, got, curv = operate(direction, [residual * pre])
    rz = got[0]
    alpha = rz / curv
    solution = solution + alpha * direction
    residual = residual - alpha * image
    for step in range(1, ITERS):
        pre = residual / cam_diag
        image_pre, got, energy = operate(pre, [residual * pre, pre * image])
        new_rz = got[0]
        beta = new_rz / rz
        direction = pre + beta * direction
        image = image_pre + beta * image
        curv = energy + beta * (2.0 * got[1] + beta * curv)
        alpha = new_rz / curv
        rz = new_rz
        solution = solution + alpha * direction
        residual = residual - alpha * image
    return (solution, residual)


def solution(mesh):
    SIZES.update(mesh.shape)
    return jax.shard_map(
        on_device,
        mesh=mesh,
        in_specs=(
            P(None, None, ("groups", "pts", "cam")),
            P(None, None, ("groups", "pts", "cam")),
            P(("groups", "pts", "cam")),
            P(("groups", "pts", "cam")),
            P(("groups", "pts")),
            P(("groups", "cam")),
            P(None, ("groups", "cam")),
        ),
        out_specs=(P(None, ("groups", "cam")), P(None, ("groups", "cam"))),
        check_vma=False,
    )
```

```python
import jax
import jax.numpy as jnp
from jax import lax
from jax.sharding import PartitionSpec as P

ITERS = 3

BF = jnp.bfloat16
F32 = jnp.float32


def split_of(count):
    lo = 1 << (max(count.bit_length() - 1, 0) // 2)
    while count % lo:
        lo //= 2
    return count // lo, lo


def pieces(value):
    first = lax.reduce_precision(value, exponent_bits=8, mantissa_bits=7)
    rest = value - first
    second = lax.reduce_precision(rest, exponent_bits=8, mantissa_bits=7)
    third = rest - second
    return first.astype(BF), second.astype(BF), third.astype(BF)


class Index:
    def __init__(self, index, count):
        self.count = count
        self.hi, self.lo = split_of(count)
        high = index // self.lo
        low = index % self.lo
        hot = (lax.broadcasted_iota(jnp.int32, (self.hi, index.shape[0]), 0) == high[None, :])
        self.hot = hot.astype(BF)
        self.hot3 = jnp.concatenate([self.hot] * 3, axis=1)
        self.hot3t = jnp.concatenate([self.hot] * 3, axis=0)
        self.low = lax.broadcasted_iota(jnp.int32, (self.lo, index.shape[0]), 0) == low[None, :]

    def segsum(self, terms):
        ncol = terms.shape[0]
        parts = [
            jnp.where(self.low[None], part[:, None, :], jnp.zeros((), BF)).reshape(ncol * self.lo, -1)
            for part in pieces(terms)
        ]
        spread = jnp.concatenate(parts, axis=1)
        out = lax.dot_general(
            self.hot3, spread, (((1,), (1,)), ((), ())), preferred_element_type=F32
        )
        return out.reshape(self.hi, ncol, self.lo).transpose(1, 0, 2).reshape(ncol, self.count)

    def gather(self, table):
        ncol = table.shape[0]
        mat = table.reshape(ncol, self.hi, self.lo).transpose(0, 2, 1).reshape(ncol * self.lo, self.hi)
        stacked = jnp.concatenate(pieces(mat), axis=1)
        spread = lax.dot_general(
            stacked, self.hot3t, (((1,), (0,)), ((), ())), preferred_element_type=F32
        ).reshape(ncol, self.lo, -1)
        return jnp.sum(jnp.where(self.low[None], spread, 0.0), axis=1)


def invert3(mat):
    c00 = mat[1, 1] * mat[2, 2] - mat[1, 2] * mat[2, 1]
    c01 = mat[0, 2] * mat[2, 1] - mat[0, 1] * mat[2, 2]
    c02 = mat[0, 1] * mat[1, 2] - mat[0, 2] * mat[1, 1]
    c10 = mat[1, 2] * mat[2, 0] - mat[1, 0] * mat[2, 2]
    c11 = mat[0, 0] * mat[2, 2] - mat[0, 2] * mat[2, 0]
    c12 = mat[0, 2] * mat[1, 0] - mat[0, 0] * mat[1, 2]
    c20 = mat[1, 0] * mat[2, 1] - mat[1, 1] * mat[2, 0]
    c21 = mat[0, 1] * mat[2, 0] - mat[0, 0] * mat[2, 1]
    c22 = mat[0, 0] * mat[1, 1] - mat[0, 1] * mat[1, 0]
    det = mat[0, 0] * c00 + mat[0, 1] * c10 + mat[0, 2] * c20
    adj = jnp.stack(
        [jnp.stack([c00, c01, c02]), jnp.stack([c10, c11, c12]), jnp.stack([c20, c21, c22])]
    )
    return adj / det


def normal_six(point_jac):
    pairs = [(0, 0), (0, 1), (0, 2), (1, 1), (1, 2), (2, 2)]
    return jnp.stack(
        [jnp.sum(point_jac[:, first] * point_jac[:, second], axis=0) for first, second in pairs]
    )


def expand_six(six):
    return jnp.stack(
        [
            jnp.stack([six[0], six[1], six[2]]),
            jnp.stack([six[1], six[3], six[4]]),
            jnp.stack([six[2], six[4], six[5]]),
        ]
    )


def point_inverse(six, damp):
    mat = expand_six(six) + damp[None, None, :] * jnp.eye(3, dtype=jnp.float32)[:, :, None]
    return invert3(mat)


SIZES = {}


def allsum(value, axis):
    size = SIZES[axis]
    if size == 4 and axis == "cam":
        peers = [
            lax.ppermute(value, axis, [(i, i ^ mask) for i in range(size)]) for mask in (1, 2, 3)
        ]
        return (value + peers[0]) + (peers[1] + peers[2])
    if size & (size - 1):
        return lax.psum(value, axis)
    step = 1
    while step < size:
        value = value + lax.ppermute(value, axis, [(i, i ^ step) for i in range(size)])
        step *= 2
    return value


def norm_sum(value):
    return allsum(value, "cam")


def on_device(cam_jac, point_jac, obs_cam, obs_point, point_damp, cam_damp, reduced_rhs):
    npts = point_damp.shape[0]
    ncam = reduced_rhs.shape[1]
    by_point = Index(obs_point, npts)
    by_cam = Index(obs_cam, ncam)
    six_terms = allsum(by_point.segsum(normal_six(point_jac)), "cam")
    inv = point_inverse(six_terms, point_damp)
    diag_terms = by_cam.segsum(jnp.sum(cam_jac * cam_jac, axis=0))
    cam_diag = allsum(diag_terms, "pts") + cam_damp[None, :]

    def as_row(rows, width):
        flat = rows.reshape(-1)
        count = -(-flat.shape[0] // width)
        return jnp.pad(flat, (0, count * width - flat.shape[0])).reshape(count, width)

    def lanes(terms):
        return jnp.sum(terms.reshape(-1, ncam), axis=0)

    def operate(vec, extras):
        y = jnp.sum(cam_jac * by_cam.gather(vec)[None], axis=1)
        u_part = by_point.segsum(jnp.sum(point_jac * y[:, None, :], axis=0))
        extras = jnp.stack([lanes(t) for t in extras] + [lanes(cam_damp[None, :] * vec * vec), lanes(y * y)])
        count = extras.shape[0]
        rows = as_row(extras, npts)
        u_all = allsum(jnp.concatenate([u_part, rows], axis=0), "cam")
        u = u_all[:3]
        got = jnp.sum(u_all[3:].reshape(-1)[: count * ncam].reshape(count, ncam), axis=1, keepdims=True)
        w = jnp.sum(inv * u[None, :, :], axis=1)
        pt_terms = jnp.sum(u * w, axis=0).reshape(-1, ncam)
        pt_row = u_all[3:].reshape(-1)[(count - 1) * ncam : count * ncam] - jnp.sum(pt_terms, axis=0)
        z = y - jnp.sum(point_jac * by_point.gather(w)[None], axis=1)
        img_part = by_cam.segsum(jnp.sum(cam_jac * z[:, None, :], axis=0))
        img_all = allsum(jnp.concatenate([img_part, pt_row[None]], axis=0), "pts")
        image = cam_damp[None, :] * vec + img_all[:-1]
        energy = got[count - 2 : count - 1] + jnp.sum(img_all[-1:], axis=1, keepdims=True)
        return image, got, energy

    solution = jnp.zeros_like(reduced_rhs)
    residual = reduced_rhs
    pre = residual / cam_diag
    direction = pre
    image, got, curv = operate(direction, [residual * pre])
    rz = got[0:1]
    alpha = rz / curv
    solution = solution + alpha * direction
    residual = residual - alpha * image
    for step in range(1, ITERS):
        pre = residual / cam_diag
        image_pre, got, energy = operate(pre, [residual * pre, pre * image])
        new_rz = got[0:1]
        beta = new_rz / rz
        direction = pre + beta * direction
        image = image_pre + beta * image
        curv = energy + beta * (2.0 * got[1:2] + beta * curv)
        alpha = new_rz / curv
        rz = new_rz
        solution = solution + alpha * direction
        residual = residual - alpha * image
    return (solution, residual)


def solution(mesh):
    SIZES.update(mesh.shape)
    return jax.shard_map(
        on_device,
        mesh=mesh,
        in_specs=(
            P(None, None, ("groups", "pts", "cam")),
            P(None, None, ("groups", "pts", "cam")),
            P(("groups", "pts", "cam")),
            P(("groups", "pts", "cam")),
            P(("groups", "pts")),
            P(("groups", "cam")),
            P(None, ("groups", "cam")),
        ),
        out_specs=(P(None, ("groups", "cam")), P(None, ("groups", "cam"))),
        check_vma=False,
    )
```

```python
import jax
import jax.numpy as jnp
from jax import lax
from jax.sharding import PartitionSpec as P

ITERS = 3

BF = jnp.bfloat16
F32 = jnp.float32


def split_of(count):
    lo = 1 << (max(count.bit_length() - 1, 0) // 2)
    while count % lo:
        lo //= 2
    return count // lo, lo


def pieces(value):
    first = lax.reduce_precision(value, exponent_bits=8, mantissa_bits=7)
    rest = value - first
    second = lax.reduce_precision(rest, exponent_bits=8, mantissa_bits=7)
    third = rest - second
    return first.astype(BF), second.astype(BF), third.astype(BF)


class Index:
    def __init__(self, index, count):
        self.count = count
        self.hi, self.lo = split_of(count)
        high = index // self.lo
        low = index % self.lo
        hot = (lax.broadcasted_iota(jnp.int32, (self.hi, index.shape[0]), 0) == high[None, :])
        self.hot = hot.astype(BF)
        self.hot3 = jnp.concatenate([self.hot] * 3, axis=1)
        self.hot3t = jnp.concatenate([self.hot] * 3, axis=0)
        self.low = lax.broadcasted_iota(jnp.int32, (self.lo, index.shape[0]), 0) == low[None, :]

    def segsum(self, terms):
        ncol = terms.shape[0]
        parts = [
            jnp.where(self.low[None], part[:, None, :], jnp.zeros((), BF)).reshape(ncol * self.lo, -1)
            for part in pieces(terms)
        ]
        spread = jnp.concatenate(parts, axis=1)
        out = lax.dot_general(
            self.hot3, spread, (((1,), (1,)), ((), ())), preferred_element_type=F32
        )
        return out.reshape(self.hi, ncol, self.lo).transpose(1, 0, 2).reshape(ncol, self.count)

    def gather(self, table):
        ncol = table.shape[0]
        mat = table.reshape(ncol, self.hi, self.lo).transpose(0, 2, 1).reshape(ncol * self.lo, self.hi)
        stacked = jnp.concatenate(pieces(mat), axis=1)
        spread = lax.dot_general(
            stacked, self.hot3t, (((1,), (0,)), ((), ())), preferred_element_type=F32
        ).reshape(ncol, self.lo, -1)
        return jnp.sum(jnp.where(self.low[None], spread, 0.0), axis=1)


def invert3(mat):
    c00 = mat[1, 1] * mat[2, 2] - mat[1, 2] * mat[2, 1]
    c01 = mat[0, 2] * mat[2, 1] - mat[0, 1] * mat[2, 2]
    c02 = mat[0, 1] * mat[1, 2] - mat[0, 2] * mat[1, 1]
    c10 = mat[1, 2] * mat[2, 0] - mat[1, 0] * mat[2, 2]
    c11 = mat[0, 0] * mat[2, 2] - mat[0, 2] * mat[2, 0]
    c12 = mat[0, 2] * mat[1, 0] - mat[0, 0] * mat[1, 2]
    c20 = mat[1, 0] * mat[2, 1] - mat[1, 1] * mat[2, 0]
    c21 = mat[0, 1] * mat[2, 0] - mat[0, 0] * mat[2, 1]
    c22 = mat[0, 0] * mat[1, 1] - mat[0, 1] * mat[1, 0]
    det = mat[0, 0] * c00 + mat[0, 1] * c10 + mat[0, 2] * c20
    adj = jnp.stack(
        [jnp.stack([c00, c01, c02]), jnp.stack([c10, c11, c12]), jnp.stack([c20, c21, c22])]
    )
    return adj / det


def normal_six(point_jac):
    pairs = [(0, 0), (0, 1), (0, 2), (1, 1), (1, 2), (2, 2)]
    return jnp.stack(
        [jnp.sum(point_jac[:, first] * point_jac[:, second], axis=0) for first, second in pairs]
    )


def expand_six(six):
    return jnp.stack(
        [
            jnp.stack([six[0], six[1], six[2]]),
            jnp.stack([six[1], six[3], six[4]]),
            jnp.stack([six[2], six[4], six[5]]),
        ]
    )


def point_inverse(six, damp):
    mat = expand_six(six) + damp[None, None, :] * jnp.eye(3, dtype=jnp.float32)[:, :, None]
    return invert3(mat)


SIZES = {}


def allsum(value, axis):
    size = SIZES[axis]
    if size == 4 and axis == "cam":
        peers = [
            lax.ppermute(value, axis, [(i, i ^ mask) for i in range(size)]) for mask in (1, 2, 3)
        ]
        return (value + peers[0]) + (peers[1] + peers[2])
    if size & (size - 1):
        return lax.psum(value, axis)
    step = 1
    while step < size:
        value = value + lax.ppermute(value, axis, [(i, i ^ step) for i in range(size)])
        step *= 2
    return value


def norm_sum(value):
    return allsum(value, "cam")


def on_device(cam_jac, point_jac, obs_cam, obs_point, point_damp, cam_damp, reduced_rhs):
    npts = point_damp.shape[0]
    ncam = reduced_rhs.shape[1]
    by_point = Index(obs_point, npts)
    by_cam = Index(obs_cam, ncam)
    six_terms = allsum(by_point.segsum(normal_six(point_jac)), "cam")
    inv = point_inverse(six_terms, point_damp)
    diag_terms = by_cam.segsum(jnp.sum(cam_jac * cam_jac, axis=0))
    cam_diag = allsum(diag_terms, "pts") + cam_damp[None, :]

    def as_row(rows, width):
        flat = rows.reshape(-1)
        count = -(-flat.shape[0] // width)
        return jnp.pad(flat, (0, count * width - flat.shape[0])).reshape(count, width)

    def lanes(terms):
        return jnp.broadcast_to(jnp.sum(terms), (ncam,))

    def operate(vec, extras):
        y = jnp.sum(cam_jac * by_cam.gather(vec)[None], axis=1)
        u_part = by_point.segsum(jnp.sum(point_jac * y[:, None, :], axis=0))
        extras = jnp.stack([lanes(t) for t in extras] + [lanes(cam_damp[None, :] * vec * vec), lanes(y * y)])
        count = extras.shape[0]
        rows = as_row(extras, npts)
        u_all = allsum(jnp.concatenate([u_part, rows], axis=0), "cam")
        u = u_all[:3]
        got = u_all[3:].reshape(-1)[: count * ncam].reshape(count, ncam)
        w = jnp.sum(inv * u[None, :, :], axis=1)
        pt_row = got[count - 1] - lanes(u * w)
        z = y - jnp.sum(point_jac * by_point.gather(w)[None], axis=1)
        img_part = by_cam.segsum(jnp.sum(cam_jac * z[:, None, :], axis=0))
        img_all = allsum(jnp.concatenate([img_part, pt_row[None]], axis=0), "pts")
        image = cam_damp[None, :] * vec + img_all[:-1]
        energy = got[count - 2] + img_all[-1]
        return image, got, energy

    solution = jnp.zeros_like(reduced_rhs)
    residual = reduced_rhs
    pre = residual / cam_diag
    direction = pre
    image, got, curv = operate(direction, [residual * pre])
    rz = got[0]
    alpha = rz / curv
    solution = solution + alpha * direction
    residual = residual - alpha * image
    for step in range(1, ITERS):
        pre = residual / cam_diag
        image_pre, got, energy = operate(pre, [residual * pre, pre * image])
        new_rz = got[0]
        beta = new_rz / rz
        direction = pre + beta * direction
        image = image_pre + beta * image
        curv = energy + beta * (2.0 * got[1] + beta * curv)
        alpha = new_rz / curv
        rz = new_rz
        solution = solution + alpha * direction
        residual = residual - alpha * image
    return (solution, residual)


def solution(mesh):
    SIZES.update(mesh.shape)
    return jax.shard_map(
        on_device,
        mesh=mesh,
        in_specs=(
            P(None, None, ("groups", "pts", "cam")),
            P(None, None, ("groups", "pts", "cam")),
            P(("groups", "pts", "cam")),
            P(("groups", "pts", "cam")),
            P(("groups", "pts")),
            P(("groups", "cam")),
            P(None, ("groups", "cam")),
        ),
        out_specs=(P(None, ("groups", "cam")), P(None, ("groups", "cam"))),
        check_vma=False,
    )
```

```python
import jax
import jax.numpy as jnp
from jax import lax
from jax.sharding import PartitionSpec as P

ITERS = 3

BF = jnp.bfloat16
F32 = jnp.float32


def split_of(count):
    lo = 1 << max((count.bit_length() - 1) // 2 - 1, 0)
    while count % lo:
        lo //= 2
    return count // lo, lo


def pieces(value):
    first = lax.reduce_precision(value, exponent_bits=8, mantissa_bits=7)
    rest = value - first
    second = lax.reduce_precision(rest, exponent_bits=8, mantissa_bits=7)
    third = rest - second
    return first.astype(BF), second.astype(BF), third.astype(BF)


class Index:
    def __init__(self, index, count):
        self.count = count
        self.hi, self.lo = split_of(count)
        high = index // self.lo
        low = index % self.lo
        hot = (lax.broadcasted_iota(jnp.int32, (self.hi, index.shape[0]), 0) == high[None, :])
        self.hot = hot.astype(BF)
        self.hot3 = jnp.concatenate([self.hot] * 3, axis=1)
        self.hot3t = jnp.concatenate([self.hot] * 3, axis=0)
        self.low = lax.broadcasted_iota(jnp.int32, (self.lo, index.shape[0]), 0) == low[None, :]

    def segsum(self, terms):
        ncol = terms.shape[0]
        parts = [
            jnp.where(self.low[None], part[:, None, :], jnp.zeros((), BF)).reshape(ncol * self.lo, -1)
            for part in pieces(terms)
        ]
        spread = jnp.concatenate(parts, axis=1)
        out = lax.dot_general(
            self.hot3, spread, (((1,), (1,)), ((), ())), preferred_element_type=F32
        )
        return out.reshape(self.hi, ncol, self.lo).transpose(1, 0, 2).reshape(ncol, self.count)

    def gather(self, table):
        ncol = table.shape[0]
        mat = table.reshape(ncol, self.hi, self.lo).transpose(0, 2, 1).reshape(ncol * self.lo, self.hi)
        stacked = jnp.concatenate(pieces(mat), axis=1)
        spread = lax.dot_general(
            stacked, self.hot3t, (((1,), (0,)), ((), ())), preferred_element_type=F32
        ).reshape(ncol, self.lo, -1)
        return jnp.sum(jnp.where(self.low[None], spread, 0.0), axis=1)


def invert3(mat):
    c00 = mat[1, 1] * mat[2, 2] - mat[1, 2] * mat[2, 1]
    c01 = mat[0, 2] * mat[2, 1] - mat[0, 1] * mat[2, 2]
    c02 = mat[0, 1] * mat[1, 2] - mat[0, 2] * mat[1, 1]
    c10 = mat[1, 2] * mat[2, 0] - mat[1, 0] * mat[2, 2]
    c11 = mat[0, 0] * mat[2, 2] - mat[0, 2] * mat[2, 0]
    c12 = mat[0, 2] * mat[1, 0] - mat[0, 0] * mat[1, 2]
    c20 = mat[1, 0] * mat[2, 1] - mat[1, 1] * mat[2, 0]
    c21 = mat[0, 1] * mat[2, 0] - mat[0, 0] * mat[2, 1]
    c22 = mat[0, 0] * mat[1, 1] - mat[0, 1] * mat[1, 0]
    det = mat[0, 0] * c00 + mat[0, 1] * c10 + mat[0, 2] * c20
    adj = jnp.stack(
        [jnp.stack([c00, c01, c02]), jnp.stack([c10, c11, c12]), jnp.stack([c20, c21, c22])]
    )
    return adj / det


def normal_six(point_jac):
    pairs = [(0, 0), (0, 1), (0, 2), (1, 1), (1, 2), (2, 2)]
    return jnp.stack(
        [jnp.sum(point_jac[:, first] * point_jac[:, second], axis=0) for first, second in pairs]
    )


def expand_six(six):
    return jnp.stack(
        [
            jnp.stack([six[0], six[1], six[2]]),
            jnp.stack([six[1], six[3], six[4]]),
            jnp.stack([six[2], six[4], six[5]]),
        ]
    )


def point_inverse(six, damp):
    mat = expand_six(six) + damp[None, None, :] * jnp.eye(3, dtype=jnp.float32)[:, :, None]
    return invert3(mat)


SIZES = {}


def allsum(value, axis):
    size = SIZES[axis]
    if size == 4 and axis == "cam":
        peers = [
            lax.ppermute(value, axis, [(i, i ^ mask) for i in range(size)]) for mask in (1, 2, 3)
        ]
        return (value + peers[0]) + (peers[1] + peers[2])
    if size & (size - 1):
        return lax.psum(value, axis)
    step = 1
    while step < size:
        value = value + lax.ppermute(value, axis, [(i, i ^ step) for i in range(size)])
        step *= 2
    return value


def norm_sum(value):
    return allsum(value, "cam")


def on_device(cam_jac, point_jac, obs_cam, obs_point, point_damp, cam_damp, reduced_rhs):
    npts = point_damp.shape[0]
    ncam = reduced_rhs.shape[1]
    by_point = Index(obs_point, npts)
    by_cam = Index(obs_cam, ncam)
    six_terms = allsum(by_point.segsum(normal_six(point_jac)), "cam")
    inv = point_inverse(six_terms, point_damp)
    diag_terms = by_cam.segsum(jnp.sum(cam_jac * cam_jac, axis=0))
    cam_diag = allsum(diag_terms, "pts") + cam_damp[None, :]

    def as_row(rows, width):
        flat = rows.reshape(-1)
        count = -(-flat.shape[0] // width)
        return jnp.pad(flat, (0, count * width - flat.shape[0])).reshape(count, width)

    def lanes(terms):
        return jnp.sum(terms.reshape(-1, ncam), axis=0)

    def operate(vec, extras):
        y = jnp.sum(cam_jac * by_cam.gather(vec)[None], axis=1)
        u_part = by_point.segsum(jnp.sum(point_jac * y[:, None, :], axis=0))
        extras = jnp.stack([lanes(t) for t in extras] + [lanes(cam_damp[None, :] * vec * vec), lanes(y * y)])
        count = extras.shape[0]
        rows = as_row(extras, npts)
        u_all = allsum(jnp.concatenate([u_part, rows], axis=0), "cam")
        u = u_all[:3]
        got = jnp.sum(u_all[3:].reshape(-1)[: count * ncam].reshape(count, ncam), axis=1, keepdims=True)
        w = jnp.sum(inv * u[None, :, :], axis=1)
        pt_terms = jnp.sum(u * w, axis=0).reshape(-1, ncam)
        pt_row = u_all[3:].reshape(-1)[(count - 1) * ncam : count * ncam] - jnp.sum(pt_terms, axis=0)
        z = y - jnp.sum(point_jac * by_point.gather(w)[None], axis=1)
        img_part = by_cam.segsum(jnp.sum(cam_jac * z[:, None, :], axis=0))
        img_all = allsum(jnp.concatenate([img_part, pt_row[None]], axis=0), "pts")
        image = cam_damp[None, :] * vec + img_all[:-1]
        energy = got[count - 2 : count - 1] + jnp.sum(img_all[-1:], axis=1, keepdims=True)
        return image, got, energy

    solution = jnp.zeros_like(reduced_rhs)
    residual = reduced_rhs
    pre = residual / cam_diag
    direction = pre
    image, got, curv = operate(direction, [residual * pre])
    rz = got[0:1]
    alpha = rz / curv
    solution = solution + alpha * direction
    residual = residual - alpha * image
    for step in range(1, ITERS):
        pre = residual / cam_diag
        image_pre, got, energy = operate(pre, [residual * pre, pre * image])
        new_rz = got[0:1]
        beta = new_rz / rz
        direction = pre + beta * direction
        image = image_pre + beta * image
        curv = energy + beta * (2.0 * got[1:2] + beta * curv)
        alpha = new_rz / curv
        rz = new_rz
        solution = solution + alpha * direction
        residual = residual - alpha * image
    return (solution, residual)


def solution(mesh):
    SIZES.update(mesh.shape)
    return jax.shard_map(
        on_device,
        mesh=mesh,
        in_specs=(
            P(None, None, ("groups", "pts", "cam")),
            P(None, None, ("groups", "pts", "cam")),
            P(("groups", "pts", "cam")),
            P(("groups", "pts", "cam")),
            P(("groups", "pts")),
            P(("groups", "cam")),
            P(None, ("groups", "cam")),
        ),
        out_specs=(P(None, ("groups", "cam")), P(None, ("groups", "cam"))),
        check_vma=False,
    )
```

```python
import jax
import jax.numpy as jnp
from jax import lax
from jax.sharding import PartitionSpec as P

ITERS = 3

BF = jnp.bfloat16
F32 = jnp.float32


def split_of(count):
    lo = 1 << max((count.bit_length() - 1) // 2 - 2, 0)
    while count % lo:
        lo //= 2
    return count // lo, lo


def pieces(value):
    first = lax.reduce_precision(value, exponent_bits=8, mantissa_bits=7)
    rest = value - first
    second = lax.reduce_precision(rest, exponent_bits=8, mantissa_bits=7)
    third = rest - second
    return first.astype(BF), second.astype(BF), third.astype(BF)


class Index:
    def __init__(self, index, count):
        self.count = count
        self.hi, self.lo = split_of(count)
        high = index // self.lo
        low = index % self.lo
        hot = (lax.broadcasted_iota(jnp.int32, (self.hi, index.shape[0]), 0) == high[None, :])
        self.hot = hot.astype(BF)
        self.hot3 = jnp.concatenate([self.hot] * 3, axis=1)
        self.hot3t = jnp.concatenate([self.hot] * 3, axis=0)
        self.low = lax.broadcasted_iota(jnp.int32, (self.lo, index.shape[0]), 0) == low[None, :]

    def segsum(self, terms):
        ncol = terms.shape[0]
        parts = [
            jnp.where(self.low[None], part[:, None, :], jnp.zeros((), BF)).reshape(ncol * self.lo, -1)
            for part in pieces(terms)
        ]
        spread = jnp.concatenate(parts, axis=1)
        out = lax.dot_general(
            self.hot3, spread, (((1,), (1,)), ((), ())), preferred_element_type=F32
        )
        return out.reshape(self.hi, ncol, self.lo).transpose(1, 0, 2).reshape(ncol, self.count)

    def gather(self, table):
        ncol = table.shape[0]
        mat = table.reshape(ncol, self.hi, self.lo).transpose(0, 2, 1).reshape(ncol * self.lo, self.hi)
        stacked = jnp.concatenate(pieces(mat), axis=1)
        spread = lax.dot_general(
            stacked, self.hot3t, (((1,), (0,)), ((), ())), preferred_element_type=F32
        ).reshape(ncol, self.lo, -1)
        return jnp.sum(jnp.where(self.low[None], spread, 0.0), axis=1)


def invert3(mat):
    c00 = mat[1, 1] * mat[2, 2] - mat[1, 2] * mat[2, 1]
    c01 = mat[0, 2] * mat[2, 1] - mat[0, 1] * mat[2, 2]
    c02 = mat[0, 1] * mat[1, 2] - mat[0, 2] * mat[1, 1]
    c10 = mat[1, 2] * mat[2, 0] - mat[1, 0] * mat[2, 2]
    c11 = mat[0, 0] * mat[2, 2] - mat[0, 2] * mat[2, 0]
    c12 = mat[0, 2] * mat[1, 0] - mat[0, 0] * mat[1, 2]
    c20 = mat[1, 0] * mat[2, 1] - mat[1, 1] * mat[2, 0]
    c21 = mat[0, 1] * mat[2, 0] - mat[0, 0] * mat[2, 1]
    c22 = mat[0, 0] * mat[1, 1] - mat[0, 1] * mat[1, 0]
    det = mat[0, 0] * c00 + mat[0, 1] * c10 + mat[0, 2] * c20
    adj = jnp.stack(
        [jnp.stack([c00, c01, c02]), jnp.stack([c10, c11, c12]), jnp.stack([c20, c21, c22])]
    )
    return adj / det


def normal_six(point_jac):
    pairs = [(0, 0), (0, 1), (0, 2), (1, 1), (1, 2), (2, 2)]
    return jnp.stack(
        [jnp.sum(point_jac[:, first] * point_jac[:, second], axis=0) for first, second in pairs]
    )


def expand_six(six):
    return jnp.stack(
        [
            jnp.stack([six[0], six[1], six[2]]),
            jnp.stack([six[1], six[3], six[4]]),
            jnp.stack([six[2], six[4], six[5]]),
        ]
    )


def point_inverse(six, damp):
    mat = expand_six(six) + damp[None, None, :] * jnp.eye(3, dtype=jnp.float32)[:, :, None]
    return invert3(mat)


SIZES = {}


def allsum(value, axis):
    size = SIZES[axis]
    if size == 4 and axis == "cam":
        peers = [
            lax.ppermute(value, axis, [(i, i ^ mask) for i in range(size)]) for mask in (1, 2, 3)
        ]
        return (value + peers[0]) + (peers[1] + peers[2])
    if size & (size - 1):
        return lax.psum(value, axis)
    step = 1
    while step < size:
        value = value + lax.ppermute(value, axis, [(i, i ^ step) for i in range(size)])
        step *= 2
    return value


def norm_sum(value):
    return allsum(value, "cam")


def on_device(cam_jac, point_jac, obs_cam, obs_point, point_damp, cam_damp, reduced_rhs):
    npts = point_damp.shape[0]
    ncam = reduced_rhs.shape[1]
    by_point = Index(obs_point, npts)
    by_cam = Index(obs_cam, ncam)
    six_terms = allsum(by_point.segsum(normal_six(point_jac)), "cam")
    inv = point_inverse(six_terms, point_damp)
    diag_terms = by_cam.segsum(jnp.sum(cam_jac * cam_jac, axis=0))
    cam_diag = allsum(diag_terms, "pts") + cam_damp[None, :]

    def as_row(rows, width):
        flat = rows.reshape(-1)
        count = -(-flat.shape[0] // width)
        return jnp.pad(flat, (0, count * width - flat.shape[0])).reshape(count, width)

    def lanes(terms):
        return jnp.sum(terms.reshape(-1, ncam), axis=0)

    def operate(vec, extras):
        y = jnp.sum(cam_jac * by_cam.gather(vec)[None], axis=1)
        u_part = by_point.segsum(jnp.sum(point_jac * y[:, None, :], axis=0))
        extras = jnp.stack([lanes(t) for t in extras] + [lanes(cam_damp[None, :] * vec * vec), lanes(y * y)])
        count = extras.shape[0]
        rows = as_row(extras, npts)
        u_all = allsum(jnp.concatenate([u_part, rows], axis=0), "cam")
        u = u_all[:3]
        got = jnp.sum(u_all[3:].reshape(-1)[: count * ncam].reshape(count, ncam), axis=1, keepdims=True)
        w = jnp.sum(inv * u[None, :, :], axis=1)
        pt_terms = jnp.sum(u * w, axis=0).reshape(-1, ncam)
        pt_row = u_all[3:].reshape(-1)[(count - 1) * ncam : count * ncam] - jnp.sum(pt_terms, axis=0)
        z = y - jnp.sum(point_jac * by_point.gather(w)[None], axis=1)
        img_part = by_cam.segsum(jnp.sum(cam_jac * z[:, None, :], axis=0))
        img_all = allsum(jnp.concatenate([img_part, pt_row[None]], axis=0), "pts")
        image = cam_damp[None, :] * vec + img_all[:-1]
        energy = got[count - 2 : count - 1] + jnp.sum(img_all[-1:], axis=1, keepdims=True)
        return image, got, energy

    solution = jnp.zeros_like(reduced_rhs)
    residual = reduced_rhs
    pre = residual / cam_diag
    direction = pre
    image, got, curv = operate(direction, [residual * pre])
    rz = got[0:1]
    alpha = rz / curv
    solution = solution + alpha * direction
    residual = residual - alpha * image
    for step in range(1, ITERS):
        pre = residual / cam_diag
        image_pre, got, energy = operate(pre, [residual * pre, pre * image])
        new_rz = got[0:1]
        beta = new_rz / rz
        direction = pre + beta * direction
        image = image_pre + beta * image
        curv = energy + beta * (2.0 * got[1:2] + beta * curv)
        alpha = new_rz / curv
        rz = new_rz
        solution = solution + alpha * direction
        residual = residual - alpha * image
    return (solution, residual)


def solution(mesh):
    SIZES.update(mesh.shape)
    return jax.shard_map(
        on_device,
        mesh=mesh,
        in_specs=(
            P(None, None, ("groups", "pts", "cam")),
            P(None, None, ("groups", "pts", "cam")),
            P(("groups", "pts", "cam")),
            P(("groups", "pts", "cam")),
            P(("groups", "pts")),
            P(("groups", "cam")),
            P(None, ("groups", "cam")),
        ),
        out_specs=(P(None, ("groups", "cam")), P(None, ("groups", "cam"))),
        check_vma=False,
    )
```

```python
import jax
import jax.numpy as jnp
from jax import lax
from jax.sharding import PartitionSpec as P

ITERS = 3

BF = jnp.bfloat16
F32 = jnp.float32


def split_of(count, shift):
    lo = 1 << max((count.bit_length() - 1) // 2 - shift, 0)
    while count % lo:
        lo //= 2
    return count // lo, lo


def pieces(value):
    first = lax.reduce_precision(value, exponent_bits=8, mantissa_bits=7)
    rest = value - first
    second = lax.reduce_precision(rest, exponent_bits=8, mantissa_bits=7)
    third = rest - second
    return first.astype(BF), second.astype(BF), third.astype(BF)


class Index:
    def __init__(self, index, count, shift):
        self.count = count
        self.hi, self.lo = split_of(count, shift)
        high = index // self.lo
        low = index % self.lo
        hot = (lax.broadcasted_iota(jnp.int32, (self.hi, index.shape[0]), 0) == high[None, :])
        self.hot = hot.astype(BF)
        self.hot3 = jnp.concatenate([self.hot] * 3, axis=1)
        self.hot3t = jnp.concatenate([self.hot] * 3, axis=0)
        self.low = lax.broadcasted_iota(jnp.int32, (self.lo, index.shape[0]), 0) == low[None, :]

    def segsum(self, terms):
        ncol = terms.shape[0]
        parts = [
            jnp.where(self.low[None], part[:, None, :], jnp.zeros((), BF)).reshape(ncol * self.lo, -1)
            for part in pieces(terms)
        ]
        spread = jnp.concatenate(parts, axis=1)
        out = lax.dot_general(
            self.hot3, spread, (((1,), (1,)), ((), ())), preferred_element_type=F32
        )
        return out.reshape(self.hi, ncol, self.lo).transpose(1, 0, 2).reshape(ncol, self.count)

    def gather(self, table):
        ncol = table.shape[0]
        mat = table.reshape(ncol, self.hi, self.lo).transpose(0, 2, 1).reshape(ncol * self.lo, self.hi)
        stacked = jnp.concatenate(pieces(mat), axis=1)
        spread = lax.dot_general(
            stacked, self.hot3t, (((1,), (0,)), ((), ())), preferred_element_type=F32
        ).reshape(ncol, self.lo, -1)
        return jnp.sum(jnp.where(self.low[None], spread, 0.0), axis=1)


def invert3(mat):
    c00 = mat[1, 1] * mat[2, 2] - mat[1, 2] * mat[2, 1]
    c01 = mat[0, 2] * mat[2, 1] - mat[0, 1] * mat[2, 2]
    c02 = mat[0, 1] * mat[1, 2] - mat[0, 2] * mat[1, 1]
    c10 = mat[1, 2] * mat[2, 0] - mat[1, 0] * mat[2, 2]
    c11 = mat[0, 0] * mat[2, 2] - mat[0, 2] * mat[2, 0]
    c12 = mat[0, 2] * mat[1, 0] - mat[0, 0] * mat[1, 2]
    c20 = mat[1, 0] * mat[2, 1] - mat[1, 1] * mat[2, 0]
    c21 = mat[0, 1] * mat[2, 0] - mat[0, 0] * mat[2, 1]
    c22 = mat[0, 0] * mat[1, 1] - mat[0, 1] * mat[1, 0]
    det = mat[0, 0] * c00 + mat[0, 1] * c10 + mat[0, 2] * c20
    adj = jnp.stack(
        [jnp.stack([c00, c01, c02]), jnp.stack([c10, c11, c12]), jnp.stack([c20, c21, c22])]
    )
    return adj / det


def normal_six(point_jac):
    pairs = [(0, 0), (0, 1), (0, 2), (1, 1), (1, 2), (2, 2)]
    return jnp.stack(
        [jnp.sum(point_jac[:, first] * point_jac[:, second], axis=0) for first, second in pairs]
    )


def expand_six(six):
    return jnp.stack(
        [
            jnp.stack([six[0], six[1], six[2]]),
            jnp.stack([six[1], six[3], six[4]]),
            jnp.stack([six[2], six[4], six[5]]),
        ]
    )


def point_inverse(six, damp):
    mat = expand_six(six) + damp[None, None, :] * jnp.eye(3, dtype=jnp.float32)[:, :, None]
    return invert3(mat)


SIZES = {}


def allsum(value, axis):
    size = SIZES[axis]
    if size == 4 and axis == "cam":
        peers = [
            lax.ppermute(value, axis, [(i, i ^ mask) for i in range(size)]) for mask in (1, 2, 3)
        ]
        return (value + peers[0]) + (peers[1] + peers[2])
    if size & (size - 1):
        return lax.psum(value, axis)
    step = 1
    while step < size:
        value = value + lax.ppermute(value, axis, [(i, i ^ step) for i in range(size)])
        step *= 2
    return value


def norm_sum(value):
    return allsum(value, "cam")


def on_device(cam_jac, point_jac, obs_cam, obs_point, point_damp, cam_damp, reduced_rhs):
    npts = point_damp.shape[0]
    ncam = reduced_rhs.shape[1]
    by_point = Index(obs_point, npts, 2)
    by_cam = Index(obs_cam, ncam, 1)
    six_terms = allsum(by_point.segsum(normal_six(point_jac)), "cam")
    inv = point_inverse(six_terms, point_damp)
    diag_terms = by_cam.segsum(jnp.sum(cam_jac * cam_jac, axis=0))
    cam_diag = allsum(diag_terms, "pts") + cam_damp[None, :]

    def as_row(rows, width):
        flat = rows.reshape(-1)
        count = -(-flat.shape[0] // width)
        return jnp.pad(flat, (0, count * width - flat.shape[0])).reshape(count, width)

    def lanes(terms):
        return jnp.sum(terms.reshape(-1, ncam), axis=0)

    def operate(vec, extras):
        y = jnp.sum(cam_jac * by_cam.gather(vec)[None], axis=1)
        u_part = by_point.segsum(jnp.sum(point_jac * y[:, None, :], axis=0))
        extras = jnp.stack([lanes(t) for t in extras] + [lanes(cam_damp[None, :] * vec * vec), lanes(y * y)])
        count = extras.shape[0]
        rows = as_row(extras, npts)
        u_all = allsum(jnp.concatenate([u_part, rows], axis=0), "cam")
        u = u_all[:3]
        got = jnp.sum(u_all[3:].reshape(-1)[: count * ncam].reshape(count, ncam), axis=1, keepdims=True)
        w = jnp.sum(inv * u[None, :, :], axis=1)
        pt_terms = jnp.sum(u * w, axis=0).reshape(-1, ncam)
        pt_row = u_all[3:].reshape(-1)[(count - 1) * ncam : count * ncam] - jnp.sum(pt_terms, axis=0)
        z = y - jnp.sum(point_jac * by_point.gather(w)[None], axis=1)
        img_part = by_cam.segsum(jnp.sum(cam_jac * z[:, None, :], axis=0))
        img_all = allsum(jnp.concatenate([img_part, pt_row[None]], axis=0), "pts")
        image = cam_damp[None, :] * vec + img_all[:-1]
        energy = got[count - 2 : count - 1] + jnp.sum(img_all[-1:], axis=1, keepdims=True)
        return image, got, energy

    solution = jnp.zeros_like(reduced_rhs)
    residual = reduced_rhs
    pre = residual / cam_diag
    direction = pre
    image, got, curv = operate(direction, [residual * pre])
    rz = got[0:1]
    alpha = rz / curv
    solution = solution + alpha * direction
    residual = residual - alpha * image
    for step in range(1, ITERS):
        pre = residual / cam_diag
        image_pre, got, energy = operate(pre, [residual * pre, pre * image])
        new_rz = got[0:1]
        beta = new_rz / rz
        direction = pre + beta * direction
        image = image_pre + beta * image
        curv = energy + beta * (2.0 * got[1:2] + beta * curv)
        alpha = new_rz / curv
        rz = new_rz
        solution = solution + alpha * direction
        residual = residual - alpha * image
    return (solution, residual)


def solution(mesh):
    SIZES.update(mesh.shape)
    return jax.shard_map(
        on_device,
        mesh=mesh,
        in_specs=(
            P(None, None, ("groups", "pts", "cam")),
            P(None, None, ("groups", "pts", "cam")),
            P(("groups", "pts", "cam")),
            P(("groups", "pts", "cam")),
            P(("groups", "pts")),
            P(("groups", "cam")),
            P(None, ("groups", "cam")),
        ),
        out_specs=(P(None, ("groups", "cam")), P(None, ("groups", "cam"))),
        check_vma=False,
    )
```

```python
import jax
import jax.numpy as jnp
from jax import lax
from jax.sharding import PartitionSpec as P

ITERS = 3

BF = jnp.bfloat16
F32 = jnp.float32


def split_of(count, shift):
    lo = 1 << max((count.bit_length() - 1) // 2 - shift, 0)
    while count % lo:
        lo //= 2
    return count // lo, lo


def pieces(value):
    first = lax.reduce_precision(value, exponent_bits=8, mantissa_bits=7)
    rest = value - first
    second = lax.reduce_precision(rest, exponent_bits=8, mantissa_bits=7)
    third = rest - second
    return first.astype(BF), second.astype(BF), third.astype(BF)


class Index:
    def __init__(self, index, count, shift):
        self.count = count
        self.hi, self.lo = split_of(count, shift)
        high = index // self.lo
        low = index % self.lo
        hot = (lax.broadcasted_iota(jnp.int32, (self.hi, index.shape[0]), 0) == high[None, :])
        self.hot = hot.astype(BF)
        self.hot3 = jnp.concatenate([self.hot] * 3, axis=1)
        self.hot3t = jnp.concatenate([self.hot] * 3, axis=0)
        self.low = lax.broadcasted_iota(jnp.int32, (self.lo, index.shape[0]), 0) == low[None, :]

    def segsum(self, terms):
        ncol = terms.shape[0]
        parts = [
            jnp.where(self.low[None], part[:, None, :], jnp.zeros((), BF)).reshape(ncol * self.lo, -1)
            for part in pieces(terms)
        ]
        spread = jnp.concatenate(parts, axis=1)
        out = lax.dot_general(
            self.hot3, spread, (((1,), (1,)), ((), ())), preferred_element_type=F32
        )
        return out.reshape(self.hi, ncol, self.lo).transpose(1, 0, 2).reshape(ncol, self.count)

    def gather(self, table):
        ncol = table.shape[0]
        mat = table.reshape(ncol, self.hi, self.lo).transpose(0, 2, 1).reshape(ncol * self.lo, self.hi)
        stacked = jnp.concatenate(pieces(mat), axis=1)
        spread = lax.dot_general(
            stacked, self.hot3t, (((1,), (0,)), ((), ())), preferred_element_type=F32
        ).reshape(ncol, self.lo, -1)
        return jnp.sum(jnp.where(self.low[None], spread, 0.0), axis=1)


def invert3(mat):
    c00 = mat[1, 1] * mat[2, 2] - mat[1, 2] * mat[2, 1]
    c01 = mat[0, 2] * mat[2, 1] - mat[0, 1] * mat[2, 2]
    c02 = mat[0, 1] * mat[1, 2] - mat[0, 2] * mat[1, 1]
    c10 = mat[1, 2] * mat[2, 0] - mat[1, 0] * mat[2, 2]
    c11 = mat[0, 0] * mat[2, 2] - mat[0, 2] * mat[2, 0]
    c12 = mat[0, 2] * mat[1, 0] - mat[0, 0] * mat[1, 2]
    c20 = mat[1, 0] * mat[2, 1] - mat[1, 1] * mat[2, 0]
    c21 = mat[0, 1] * mat[2, 0] - mat[0, 0] * mat[2, 1]
    c22 = mat[0, 0] * mat[1, 1] - mat[0, 1] * mat[1, 0]
    det = mat[0, 0] * c00 + mat[0, 1] * c10 + mat[0, 2] * c20
    adj = jnp.stack(
        [jnp.stack([c00, c01, c02]), jnp.stack([c10, c11, c12]), jnp.stack([c20, c21, c22])]
    )
    return adj / det


def normal_six(point_jac):
    pairs = [(0, 0), (0, 1), (0, 2), (1, 1), (1, 2), (2, 2)]
    return jnp.stack(
        [jnp.sum(point_jac[:, first] * point_jac[:, second], axis=0) for first, second in pairs]
    )


def expand_six(six):
    return jnp.stack(
        [
            jnp.stack([six[0], six[1], six[2]]),
            jnp.stack([six[1], six[3], six[4]]),
            jnp.stack([six[2], six[4], six[5]]),
        ]
    )


def point_inverse(six, damp):
    mat = expand_six(six) + damp[None, None, :] * jnp.eye(3, dtype=jnp.float32)[:, :, None]
    return invert3(mat)


SIZES = {}


def allsum(value, axis):
    size = SIZES[axis]
    if size == 4 and axis == "cam":
        peers = [
            lax.ppermute(value, axis, [(i, i ^ mask) for i in range(size)]) for mask in (1, 2, 3)
        ]
        return (value + peers[0]) + (peers[1] + peers[2])
    if size & (size - 1):
        return lax.psum(value, axis)
    step = 1
    while step < size:
        value = value + lax.ppermute(value, axis, [(i, i ^ step) for i in range(size)])
        step *= 2
    return value


def norm_sum(value):
    return allsum(value, "cam")


def on_device(cam_jac, point_jac, obs_cam, obs_point, point_damp, cam_damp, reduced_rhs):
    npts = point_damp.shape[0]
    ncam = reduced_rhs.shape[1]
    by_point = Index(obs_point, npts, 1)
    by_cam = Index(obs_cam, ncam, 0)
    six_terms = allsum(by_point.segsum(normal_six(point_jac)), "cam")
    inv = point_inverse(six_terms, point_damp)
    diag_terms = by_cam.segsum(jnp.sum(cam_jac * cam_jac, axis=0))
    cam_diag = allsum(diag_terms, "pts") + cam_damp[None, :]

    def as_row(rows, width):
        flat = rows.reshape(-1)
        count = -(-flat.shape[0] // width)
        return jnp.pad(flat, (0, count * width - flat.shape[0])).reshape(count, width)

    def lanes(terms):
        return jnp.sum(terms.reshape(-1, ncam), axis=0)

    def operate(vec, extras):
        y = jnp.sum(cam_jac * by_cam.gather(vec)[None], axis=1)
        u_part = by_point.segsum(jnp.sum(point_jac * y[:, None, :], axis=0))
        extras = jnp.stack([lanes(t) for t in extras] + [lanes(cam_damp[None, :] * vec * vec), lanes(y * y)])
        count = extras.shape[0]
        rows = as_row(extras, npts)
        u_all = allsum(jnp.concatenate([u_part, rows], axis=0), "cam")
        u = u_all[:3]
        got = jnp.sum(u_all[3:].reshape(-1)[: count * ncam].reshape(count, ncam), axis=1, keepdims=True)
        w = jnp.sum(inv * u[None, :, :], axis=1)
        pt_terms = jnp.sum(u * w, axis=0).reshape(-1, ncam)
        pt_row = u_all[3:].reshape(-1)[(count - 1) * ncam : count * ncam] - jnp.sum(pt_terms, axis=0)
        z = y - jnp.sum(point_jac * by_point.gather(w)[None], axis=1)
        img_part = by_cam.segsum(jnp.sum(cam_jac * z[:, None, :], axis=0))
        img_all = allsum(jnp.concatenate([img_part, pt_row[None]], axis=0), "pts")
        image = cam_damp[None, :] * vec + img_all[:-1]
        energy = got[count - 2 : count - 1] + jnp.sum(img_all[-1:], axis=1, keepdims=True)
        return image, got, energy

    solution = jnp.zeros_like(reduced_rhs)
    residual = reduced_rhs
    pre = residual / cam_diag
    direction = pre
    image, got, curv = operate(direction, [residual * pre])
    rz = got[0:1]
    alpha = rz / curv
    solution = solution + alpha * direction
    residual = residual - alpha * image
    for step in range(1, ITERS):
        pre = residual / cam_diag
        image_pre, got, energy = operate(pre, [residual * pre, pre * image])
        new_rz = got[0:1]
        beta = new_rz / rz
        direction = pre + beta * direction
        image = image_pre + beta * image
        curv = energy + beta * (2.0 * got[1:2] + beta * curv)
        alpha = new_rz / curv
        rz = new_rz
        solution = solution + alpha * direction
        residual = residual - alpha * image
    return (solution, residual)


def solution(mesh):
    SIZES.update(mesh.shape)
    return jax.shard_map(
        on_device,
        mesh=mesh,
        in_specs=(
            P(None, None, ("groups", "pts", "cam")),
            P(None, None, ("groups", "pts", "cam")),
            P(("groups", "pts", "cam")),
            P(("groups", "pts", "cam")),
            P(("groups", "pts")),
            P(("groups", "cam")),
            P(None, ("groups", "cam")),
        ),
        out_specs=(P(None, ("groups", "cam")), P(None, ("groups", "cam"))),
        check_vma=False,
    )
```

```python
import jax
import jax.numpy as jnp
from jax import lax
from jax.sharding import PartitionSpec as P

ITERS = 3

BF = jnp.bfloat16
F32 = jnp.float32


def split_of(count):
    lo = 1 << max((count.bit_length() - 1) // 2 - 1, 0)
    while count % lo:
        lo //= 2
    return count // lo, lo


def pieces(value):
    first = lax.reduce_precision(value, exponent_bits=8, mantissa_bits=7)
    rest = value - first
    second = lax.reduce_precision(rest, exponent_bits=8, mantissa_bits=7)
    third = rest - second
    return first.astype(BF), second.astype(BF), third.astype(BF)


class Index:
    def __init__(self, index, count):
        self.count = count
        self.hi, self.lo = split_of(count)
        high = index // self.lo
        low = index % self.lo
        hot = (lax.broadcasted_iota(jnp.int32, (self.hi, index.shape[0]), 0) == high[None, :])
        self.hot = hot.astype(BF)
        self.hot3 = jnp.concatenate([self.hot] * 3, axis=1)
        self.hot3t = jnp.concatenate([self.hot] * 3, axis=0)
        self.low = lax.broadcasted_iota(jnp.int32, (self.lo, index.shape[0]), 0) == low[None, :]

    def segsum(self, terms):
        ncol = terms.shape[0]
        parts = [
            jnp.where(self.low[None], part[:, None, :], jnp.zeros((), BF)).reshape(ncol * self.lo, -1)
            for part in pieces(terms)
        ]
        spread = jnp.concatenate(parts, axis=1)
        out = lax.dot_general(
            self.hot3, spread, (((1,), (1,)), ((), ())), preferred_element_type=F32
        )
        return out.reshape(self.hi, ncol, self.lo).transpose(1, 0, 2).reshape(ncol, self.count)

    def gather(self, table):
        ncol = table.shape[0]
        mat = table.reshape(ncol, self.hi, self.lo).transpose(0, 2, 1).reshape(ncol * self.lo, self.hi)
        stacked = jnp.concatenate(pieces(mat), axis=1)
        spread = lax.dot_general(
            stacked, self.hot3t, (((1,), (0,)), ((), ())), preferred_element_type=F32
        ).reshape(ncol, self.lo, -1)
        return jnp.sum(jnp.where(self.low[None], spread, 0.0), axis=1)


def invert3(mat):
    c00 = mat[1, 1] * mat[2, 2] - mat[1, 2] * mat[2, 1]
    c01 = mat[0, 2] * mat[2, 1] - mat[0, 1] * mat[2, 2]
    c02 = mat[0, 1] * mat[1, 2] - mat[0, 2] * mat[1, 1]
    c10 = mat[1, 2] * mat[2, 0] - mat[1, 0] * mat[2, 2]
    c11 = mat[0, 0] * mat[2, 2] - mat[0, 2] * mat[2, 0]
    c12 = mat[0, 2] * mat[1, 0] - mat[0, 0] * mat[1, 2]
    c20 = mat[1, 0] * mat[2, 1] - mat[1, 1] * mat[2, 0]
    c21 = mat[0, 1] * mat[2, 0] - mat[0, 0] * mat[2, 1]
    c22 = mat[0, 0] * mat[1, 1] - mat[0, 1] * mat[1, 0]
    det = mat[0, 0] * c00 + mat[0, 1] * c10 + mat[0, 2] * c20
    adj = jnp.stack(
        [jnp.stack([c00, c01, c02]), jnp.stack([c10, c11, c12]), jnp.stack([c20, c21, c22])]
    )
    return adj / det


def normal_six(point_jac):
    pairs = [(0, 0), (0, 1), (0, 2), (1, 1), (1, 2), (2, 2)]
    return jnp.stack(
        [jnp.sum(point_jac[:, first] * point_jac[:, second], axis=0) for first, second in pairs]
    )


def expand_six(six):
    return jnp.stack(
        [
            jnp.stack([six[0], six[1], six[2]]),
            jnp.stack([six[1], six[3], six[4]]),
            jnp.stack([six[2], six[4], six[5]]),
        ]
    )


def point_inverse(six, damp):
    mat = expand_six(six) + damp[None, None, :] * jnp.eye(3, dtype=jnp.float32)[:, :, None]
    return invert3(mat)


SIZES = {}


def allsum(value, axis):
    size = SIZES[axis]
    if size == 4 and axis == "one_round":
        peers = [
            lax.ppermute(value, axis, [(i, i ^ mask) for i in range(size)]) for mask in (1, 2, 3)
        ]
        return (value + peers[0]) + (peers[1] + peers[2])
    if size & (size - 1):
        return lax.psum(value, axis)
    step = 1
    while step < size:
        value = value + lax.ppermute(value, axis, [(i, i ^ step) for i in range(size)])
        step *= 2
    return value


def norm_sum(value):
    return allsum(value, "cam")


def on_device(cam_jac, point_jac, obs_cam, obs_point, point_damp, cam_damp, reduced_rhs):
    npts = point_damp.shape[0]
    ncam = reduced_rhs.shape[1]
    by_point = Index(obs_point, npts)
    by_cam = Index(obs_cam, ncam)
    six_terms = allsum(by_point.segsum(normal_six(point_jac)), "cam")
    inv = point_inverse(six_terms, point_damp)
    diag_terms = by_cam.segsum(jnp.sum(cam_jac * cam_jac, axis=0))
    cam_diag = allsum(diag_terms, "pts") + cam_damp[None, :]

    def as_row(rows, width):
        flat = rows.reshape(-1)
        count = -(-flat.shape[0] // width)
        return jnp.pad(flat, (0, count * width - flat.shape[0])).reshape(count, width)

    def lanes(terms):
        return jnp.sum(terms.reshape(-1, ncam), axis=0)

    def operate(vec, extras):
        y = jnp.sum(cam_jac * by_cam.gather(vec)[None], axis=1)
        u_part = by_point.segsum(jnp.sum(point_jac * y[:, None, :], axis=0))
        extras = jnp.stack([lanes(t) for t in extras] + [lanes(cam_damp[None, :] * vec * vec), lanes(y * y)])
        count = extras.shape[0]
        rows = as_row(extras, npts)
        u_all = allsum(jnp.concatenate([u_part, rows], axis=0), "cam")
        u = u_all[:3]
        got = jnp.sum(u_all[3:].reshape(-1)[: count * ncam].reshape(count, ncam), axis=1, keepdims=True)
        w = jnp.sum(inv * u[None, :, :], axis=1)
        pt_terms = jnp.sum(u * w, axis=0).reshape(-1, ncam)
        pt_row = u_all[3:].reshape(-1)[(count - 1) * ncam : count * ncam] - jnp.sum(pt_terms, axis=0)
        z = y - jnp.sum(point_jac * by_point.gather(w)[None], axis=1)
        img_part = by_cam.segsum(jnp.sum(cam_jac * z[:, None, :], axis=0))
        img_all = allsum(jnp.concatenate([img_part, pt_row[None]], axis=0), "pts")
        image = cam_damp[None, :] * vec + img_all[:-1]
        energy = got[count - 2 : count - 1] + jnp.sum(img_all[-1:], axis=1, keepdims=True)
        return image, got, energy

    solution = jnp.zeros_like(reduced_rhs)
    residual = reduced_rhs
    pre = residual / cam_diag
    direction = pre
    image, got, curv = operate(direction, [residual * pre])
    rz = got[0:1]
    alpha = rz / curv
    solution = solution + alpha * direction
    residual = residual - alpha * image
    for step in range(1, ITERS):
        pre = residual / cam_diag
        image_pre, got, energy = operate(pre, [residual * pre, pre * image])
        new_rz = got[0:1]
        beta = new_rz / rz
        direction = pre + beta * direction
        image = image_pre + beta * image
        curv = energy + beta * (2.0 * got[1:2] + beta * curv)
        alpha = new_rz / curv
        rz = new_rz
        solution = solution + alpha * direction
        residual = residual - alpha * image
    return (solution, residual)


def solution(mesh):
    SIZES.update(mesh.shape)
    return jax.shard_map(
        on_device,
        mesh=mesh,
        in_specs=(
            P(None, None, ("groups", "pts", "cam")),
            P(None, None, ("groups", "pts", "cam")),
            P(("groups", "pts", "cam")),
            P(("groups", "pts", "cam")),
            P(("groups", "pts")),
            P(("groups", "cam")),
            P(None, ("groups", "cam")),
        ),
        out_specs=(P(None, ("groups", "cam")), P(None, ("groups", "cam"))),
        check_vma=False,
    )
```

```python
import jax
import jax.numpy as jnp
from jax import lax
from jax.sharding import PartitionSpec as P

ITERS = 3

BF = jnp.bfloat16
F32 = jnp.float32


def split_of(count):
    lo = 1 << max((count.bit_length() - 1) // 2 - 1, 0)
    while count % lo:
        lo //= 2
    return count // lo, lo


def pieces(value):
    first = lax.reduce_precision(value, exponent_bits=8, mantissa_bits=7)
    rest = value - first
    second = lax.reduce_precision(rest, exponent_bits=8, mantissa_bits=7)
    third = rest - second
    return first.astype(BF), second.astype(BF), third.astype(BF)


class Index:
    def __init__(self, index, count):
        self.count = count
        self.hi, self.lo = split_of(count)
        high = index // self.lo
        low = index % self.lo
        hot = (lax.broadcasted_iota(jnp.int32, (self.hi, index.shape[0]), 0) == high[None, :])
        self.hot = hot.astype(BF)
        self.hot3 = jnp.concatenate([self.hot] * 3, axis=1)
        self.hot3t = jnp.concatenate([self.hot] * 3, axis=0)
        self.low = lax.broadcasted_iota(jnp.int32, (self.lo, index.shape[0]), 0) == low[None, :]

    def segsum(self, terms):
        ncol = terms.shape[0]
        parts = [
            jnp.where(self.low[None], part[:, None, :], jnp.zeros((), BF)).reshape(ncol * self.lo, -1)
            for part in pieces(terms)
        ]
        spread = jnp.concatenate(parts, axis=1)
        out = lax.dot_general(
            self.hot3, spread, (((1,), (1,)), ((), ())), preferred_element_type=F32
        )
        return out.reshape(self.hi, ncol, self.lo).transpose(1, 0, 2).reshape(ncol, self.count)

    def gather(self, table):
        ncol = table.shape[0]
        mat = table.reshape(ncol, self.hi, self.lo).transpose(0, 2, 1).reshape(ncol * self.lo, self.hi)
        stacked = jnp.concatenate(pieces(mat), axis=1)
        spread = lax.dot_general(
            stacked, self.hot3t, (((1,), (0,)), ((), ())), preferred_element_type=F32
        ).reshape(ncol, self.lo, -1)
        return jnp.sum(jnp.where(self.low[None], spread, 0.0), axis=1)


def invert3(mat):
    c00 = mat[1, 1] * mat[2, 2] - mat[1, 2] * mat[2, 1]
    c01 = mat[0, 2] * mat[2, 1] - mat[0, 1] * mat[2, 2]
    c02 = mat[0, 1] * mat[1, 2] - mat[0, 2] * mat[1, 1]
    c10 = mat[1, 2] * mat[2, 0] - mat[1, 0] * mat[2, 2]
    c11 = mat[0, 0] * mat[2, 2] - mat[0, 2] * mat[2, 0]
    c12 = mat[0, 2] * mat[1, 0] - mat[0, 0] * mat[1, 2]
    c20 = mat[1, 0] * mat[2, 1] - mat[1, 1] * mat[2, 0]
    c21 = mat[0, 1] * mat[2, 0] - mat[0, 0] * mat[2, 1]
    c22 = mat[0, 0] * mat[1, 1] - mat[0, 1] * mat[1, 0]
    det = mat[0, 0] * c00 + mat[0, 1] * c10 + mat[0, 2] * c20
    adj = jnp.stack(
        [jnp.stack([c00, c01, c02]), jnp.stack([c10, c11, c12]), jnp.stack([c20, c21, c22])]
    )
    return adj / det


def normal_six(point_jac):
    pairs = [(0, 0), (0, 1), (0, 2), (1, 1), (1, 2), (2, 2)]
    return jnp.stack(
        [jnp.sum(point_jac[:, first] * point_jac[:, second], axis=0) for first, second in pairs]
    )


def expand_six(six):
    return jnp.stack(
        [
            jnp.stack([six[0], six[1], six[2]]),
            jnp.stack([six[1], six[3], six[4]]),
            jnp.stack([six[2], six[4], six[5]]),
        ]
    )


def point_inverse(six, damp):
    mat = expand_six(six) + damp[None, None, :] * jnp.eye(3, dtype=jnp.float32)[:, :, None]
    return invert3(mat)


SIZES = {}


def allsum(value, axis):
    size = SIZES[axis]
    if size == 4 and axis == "one_round":
        peers = [
            lax.ppermute(value, axis, [(i, i ^ mask) for i in range(size)]) for mask in (1, 2, 3)
        ]
        return (value + peers[0]) + (peers[1] + peers[2])
    if size & (size - 1):
        return lax.psum(value, axis)
    step = 1
    while step < size:
        value = value + lax.ppermute(value, axis, [(i, i ^ step) for i in range(size)])
        step *= 2
    return value


def norm_sum(value):
    return allsum(value, "cam")


def on_device(cam_jac, point_jac, obs_cam, obs_point, point_damp, cam_damp, reduced_rhs):
    npts = point_damp.shape[0]
    ncam = reduced_rhs.shape[1]
    by_point = Index(obs_point, npts)
    by_cam = Index(obs_cam, ncam)
    six_terms = allsum(by_point.segsum(normal_six(point_jac)), "cam")
    inv = point_inverse(six_terms, point_damp)
    diag_terms = by_cam.segsum(jnp.sum(cam_jac * cam_jac, axis=0))
    cam_diag = allsum(diag_terms, "pts") + cam_damp[None, :]

    def as_row(rows, width):
        flat = rows.reshape(-1)
        count = -(-flat.shape[0] // width)
        return jnp.pad(flat, (0, count * width - flat.shape[0])).reshape(count, width)

    def lanes(terms):
        return jnp.sum(terms.reshape(-1, ncam), axis=0)

    def operate(vec, extras):
        y = jnp.sum(cam_jac * by_cam.gather(vec)[None], axis=1)
        u_part = by_point.segsum(jnp.sum(point_jac * y[:, None, :], axis=0))
        extras = jnp.stack([lanes(t) for t in extras] + [lanes(cam_damp[None, :] * vec * vec), lanes(y * y)])
        count = extras.shape[0]
        rows = as_row(extras, npts)
        u_all = allsum(jnp.concatenate([u_part, rows], axis=0), "cam")
        u = u_all[:3]
        got = jnp.sum(u_all[3:].reshape(-1)[: count * ncam].reshape(count, ncam), axis=1, keepdims=True)
        w = jnp.sum(inv * u[None, :, :], axis=1)
        pt_row = jnp.broadcast_to(got[count - 1] - jnp.sum(u * w), (ncam,))
        z = y - jnp.sum(point_jac * by_point.gather(w)[None], axis=1)
        img_part = by_cam.segsum(jnp.sum(cam_jac * z[:, None, :], axis=0))
        img_all = allsum(jnp.concatenate([img_part, pt_row[None]], axis=0), "pts")
        image = cam_damp[None, :] * vec + img_all[:-1]
        energy = got[count - 2] + img_all[-1:]
        return image, got, energy

    solution = jnp.zeros_like(reduced_rhs)
    residual = reduced_rhs
    pre = residual / cam_diag
    direction = pre
    image, got, curv = operate(direction, [residual * pre])
    rz = got[0:1]
    alpha = rz / curv
    solution = solution + alpha * direction
    residual = residual - alpha * image
    for step in range(1, ITERS):
        pre = residual / cam_diag
        image_pre, got, energy = operate(pre, [residual * pre, pre * image])
        new_rz = got[0:1]
        beta = new_rz / rz
        direction = pre + beta * direction
        image = image_pre + beta * image
        curv = energy + beta * (2.0 * got[1:2] + beta * curv)
        alpha = new_rz / curv
        rz = new_rz
        solution = solution + alpha * direction
        residual = residual - alpha * image
    return (solution, residual)


def solution(mesh):
    SIZES.update(mesh.shape)
    return jax.shard_map(
        on_device,
        mesh=mesh,
        in_specs=(
            P(None, None, ("groups", "pts", "cam")),
            P(None, None, ("groups", "pts", "cam")),
            P(("groups", "pts", "cam")),
            P(("groups", "pts", "cam")),
            P(("groups", "pts")),
            P(("groups", "cam")),
            P(None, ("groups", "cam")),
        ),
        out_specs=(P(None, ("groups", "cam")), P(None, ("groups", "cam"))),
        check_vma=False,
    )
```

```python
import jax
import jax.numpy as jnp
from jax import lax
from jax.sharding import PartitionSpec as P

ITERS = 3

BF = jnp.bfloat16
F32 = jnp.float32


def split_of(count):
    lo = 1 << max((count.bit_length() - 1) // 2 - 1, 0)
    while count % lo:
        lo //= 2
    return count // lo, lo


def pieces(value):
    first = lax.reduce_precision(value, exponent_bits=8, mantissa_bits=7)
    rest = value - first
    second = lax.reduce_precision(rest, exponent_bits=8, mantissa_bits=7)
    third = rest - second
    return first.astype(BF), second.astype(BF), third.astype(BF)


class Index:
    def __init__(self, index, count):
        self.count = count
        self.hi, self.lo = split_of(count)
        high = index // self.lo
        low = index % self.lo
        hot = (lax.broadcasted_iota(jnp.int32, (self.hi, index.shape[0]), 0) == high[None, :])
        self.hot = hot.astype(BF)
        self.hot3 = jnp.concatenate([self.hot] * 3, axis=1)
        self.hot3t = jnp.concatenate([self.hot] * 3, axis=0)
        self.low = lax.broadcasted_iota(jnp.int32, (self.lo, index.shape[0]), 0) == low[None, :]

    def segsum(self, terms):
        ncol = terms.shape[0]
        parts = [
            jnp.where(self.low[None], part[:, None, :], jnp.zeros((), BF)).reshape(ncol * self.lo, -1)
            for part in pieces(terms)
        ]
        spread = jnp.concatenate(parts, axis=1)
        out = lax.dot_general(
            self.hot3, spread, (((1,), (1,)), ((), ())), preferred_element_type=F32
        )
        return out.reshape(self.hi, ncol, self.lo).transpose(1, 0, 2).reshape(ncol, self.count)

    def gather(self, table):
        ncol = table.shape[0]
        mat = table.reshape(ncol, self.hi, self.lo).transpose(0, 2, 1).reshape(ncol * self.lo, self.hi)
        stacked = jnp.concatenate(pieces(mat), axis=1)
        spread = lax.dot_general(
            stacked, self.hot3t, (((1,), (0,)), ((), ())), preferred_element_type=F32
        ).reshape(ncol, self.lo, -1)
        return jnp.sum(jnp.where(self.low[None], spread, 0.0), axis=1)


def invert3(mat):
    c00 = mat[1, 1] * mat[2, 2] - mat[1, 2] * mat[2, 1]
    c01 = mat[0, 2] * mat[2, 1] - mat[0, 1] * mat[2, 2]
    c02 = mat[0, 1] * mat[1, 2] - mat[0, 2] * mat[1, 1]
    c10 = mat[1, 2] * mat[2, 0] - mat[1, 0] * mat[2, 2]
    c11 = mat[0, 0] * mat[2, 2] - mat[0, 2] * mat[2, 0]
    c12 = mat[0, 2] * mat[1, 0] - mat[0, 0] * mat[1, 2]
    c20 = mat[1, 0] * mat[2, 1] - mat[1, 1] * mat[2, 0]
    c21 = mat[0, 1] * mat[2, 0] - mat[0, 0] * mat[2, 1]
    c22 = mat[0, 0] * mat[1, 1] - mat[0, 1] * mat[1, 0]
    det = mat[0, 0] * c00 + mat[0, 1] * c10 + mat[0, 2] * c20
    adj = jnp.stack(
        [jnp.stack([c00, c01, c02]), jnp.stack([c10, c11, c12]), jnp.stack([c20, c21, c22])]
    )
    return adj / det


def normal_six(point_jac):
    pairs = [(0, 0), (0, 1), (0, 2), (1, 1), (1, 2), (2, 2)]
    return jnp.stack(
        [jnp.sum(point_jac[:, first] * point_jac[:, second], axis=0) for first, second in pairs]
    )


def expand_six(six):
    return jnp.stack(
        [
            jnp.stack([six[0], six[1], six[2]]),
            jnp.stack([six[1], six[3], six[4]]),
            jnp.stack([six[2], six[4], six[5]]),
        ]
    )


def point_inverse(six, damp):
    mat = expand_six(six) + damp[None, None, :] * jnp.eye(3, dtype=jnp.float32)[:, :, None]
    return invert3(mat)


SIZES = {}


def allsum(value, axis):
    size = SIZES[axis]
    if size == 4 and axis == "pts":
        peers = [
            lax.ppermute(value, axis, [(i, i ^ mask) for i in range(size)]) for mask in (1, 2, 3)
        ]
        return (value + peers[0]) + (peers[1] + peers[2])
    if size & (size - 1):
        return lax.psum(value, axis)
    step = 1
    while step < size:
        value = value + lax.ppermute(value, axis, [(i, i ^ step) for i in range(size)])
        step *= 2
    return value


def norm_sum(value):
    return allsum(value, "cam")


def on_device(cam_jac, point_jac, obs_cam, obs_point, point_damp, cam_damp, reduced_rhs):
    npts = point_damp.shape[0]
    ncam = reduced_rhs.shape[1]
    by_point = Index(obs_point, npts)
    by_cam = Index(obs_cam, ncam)
    six_terms = allsum(by_point.segsum(normal_six(point_jac)), "cam")
    inv = point_inverse(six_terms, point_damp)
    diag_terms = by_cam.segsum(jnp.sum(cam_jac * cam_jac, axis=0))
    cam_diag = allsum(diag_terms, "pts") + cam_damp[None, :]

    def as_row(rows, width):
        flat = rows.reshape(-1)
        count = -(-flat.shape[0] // width)
        return jnp.pad(flat, (0, count * width - flat.shape[0])).reshape(count, width)

    def lanes(terms):
        return jnp.sum(terms.reshape(-1, ncam), axis=0)

    def operate(vec, extras):
        y = jnp.sum(cam_jac * by_cam.gather(vec)[None], axis=1)
        u_part = by_point.segsum(jnp.sum(point_jac * y[:, None, :], axis=0))
        extras = jnp.stack([lanes(t) for t in extras] + [lanes(cam_damp[None, :] * vec * vec), lanes(y * y)])
        count = extras.shape[0]
        rows = as_row(extras, npts)
        u_all = allsum(jnp.concatenate([u_part, rows], axis=0), "cam")
        u = u_all[:3]
        got = jnp.sum(u_all[3:].reshape(-1)[: count * ncam].reshape(count, ncam), axis=1, keepdims=True)
        w = jnp.sum(inv * u[None, :, :], axis=1)
        pt_terms = jnp.sum(u * w, axis=0).reshape(-1, ncam)
        pt_row = u_all[3:].reshape(-1)[(count - 1) * ncam : count * ncam] - jnp.sum(pt_terms, axis=0)
        z = y - jnp.sum(point_jac * by_point.gather(w)[None], axis=1)
        img_part = by_cam.segsum(jnp.sum(cam_jac * z[:, None, :], axis=0))
        img_all = allsum(jnp.concatenate([img_part, pt_row[None]], axis=0), "pts")
        image = cam_damp[None, :] * vec + img_all[:-1]
        energy = got[count - 2 : count - 1] + jnp.sum(img_all[-1:], axis=1, keepdims=True)
        return image, got, energy

    solution = jnp.zeros_like(reduced_rhs)
    residual = reduced_rhs
    pre = residual / cam_diag
    direction = pre
    image, got, curv = operate(direction, [residual * pre])
    rz = got[0:1]
    alpha = rz / curv
    solution = solution + alpha * direction
    residual = residual - alpha * image
    for step in range(1, ITERS):
        pre = residual / cam_diag
        image_pre, got, energy = operate(pre, [residual * pre, pre * image])
        new_rz = got[0:1]
        beta = new_rz / rz
        direction = pre + beta * direction
        image = image_pre + beta * image
        curv = energy + beta * (2.0 * got[1:2] + beta * curv)
        alpha = new_rz / curv
        rz = new_rz
        solution = solution + alpha * direction
        residual = residual - alpha * image
    return (solution, residual)


def solution(mesh):
    SIZES.update(mesh.shape)
    return jax.shard_map(
        on_device,
        mesh=mesh,
        in_specs=(
            P(None, None, ("groups", "pts", "cam")),
            P(None, None, ("groups", "pts", "cam")),
            P(("groups", "pts", "cam")),
            P(("groups", "pts", "cam")),
            P(("groups", "pts")),
            P(("groups", "cam")),
            P(None, ("groups", "cam")),
        ),
        out_specs=(P(None, ("groups", "cam")), P(None, ("groups", "cam"))),
        check_vma=False,
    )
```

```python
import jax
import jax.numpy as jnp
from jax import lax
from jax.sharding import PartitionSpec as P

ITERS = 3

BF = jnp.bfloat16
F32 = jnp.float32


def split_of(count):
    lo = 1 << max((count.bit_length() - 1) // 2 - 1, 0)
    while count % lo:
        lo //= 2
    return count // lo, lo


def pieces(value):
    first = lax.reduce_precision(value, exponent_bits=8, mantissa_bits=7)
    rest = value - first
    second = lax.reduce_precision(rest, exponent_bits=8, mantissa_bits=7)
    third = rest - second
    return first.astype(BF), second.astype(BF), third.astype(BF)


class Index:
    def __init__(self, index, count):
        self.count = count
        self.hi, self.lo = split_of(count)
        high = index // self.lo
        low = index % self.lo
        hot = (lax.broadcasted_iota(jnp.int32, (self.hi, index.shape[0]), 0) == high[None, :])
        self.hot = hot.astype(BF)
        self.hot3 = jnp.concatenate([self.hot] * 3, axis=1)
        self.hot3t = jnp.concatenate([self.hot] * 3, axis=0)
        self.low = lax.broadcasted_iota(jnp.int32, (self.lo, index.shape[0]), 0) == low[None, :]

    def segsum(self, terms):
        ncol = terms.shape[0]
        parts = [
            jnp.where(self.low[None], part[:, None, :], jnp.zeros((), BF)).reshape(ncol * self.lo, -1)
            for part in pieces(terms)
        ]
        spread = jnp.concatenate(parts, axis=0)
        out = lax.dot_general(
            self.hot, spread, (((1,), (1,)), ((), ())), preferred_element_type=F32
        ).reshape(self.hi, 3, ncol, self.lo)
        out = (out[:, 0] + out[:, 1]) + out[:, 2]
        return out.transpose(1, 0, 2).reshape(ncol, self.count)

    def gather(self, table):
        ncol = table.shape[0]
        mat = table.reshape(ncol, self.hi, self.lo).transpose(0, 2, 1).reshape(ncol * self.lo, self.hi)
        stacked = jnp.concatenate(pieces(mat), axis=1)
        spread = lax.dot_general(
            stacked, self.hot3t, (((1,), (0,)), ((), ())), preferred_element_type=F32
        ).reshape(ncol, self.lo, -1)
        return jnp.sum(jnp.where(self.low[None], spread, 0.0), axis=1)


def invert3(mat):
    c00 = mat[1, 1] * mat[2, 2] - mat[1, 2] * mat[2, 1]
    c01 = mat[0, 2] * mat[2, 1] - mat[0, 1] * mat[2, 2]
    c02 = mat[0, 1] * mat[1, 2] - mat[0, 2] * mat[1, 1]
    c10 = mat[1, 2] * mat[2, 0] - mat[1, 0] * mat[2, 2]
    c11 = mat[0, 0] * mat[2, 2] - mat[0, 2] * mat[2, 0]
    c12 = mat[0, 2] * mat[1, 0] - mat[0, 0] * mat[1, 2]
    c20 = mat[1, 0] * mat[2, 1] - mat[1, 1] * mat[2, 0]
    c21 = mat[0, 1] * mat[2, 0] - mat[0, 0] * mat[2, 1]
    c22 = mat[0, 0] * mat[1, 1] - mat[0, 1] * mat[1, 0]
    det = mat[0, 0] * c00 + mat[0, 1] * c10 + mat[0, 2] * c20
    adj = jnp.stack(
        [jnp.stack([c00, c01, c02]), jnp.stack([c10, c11, c12]), jnp.stack([c20, c21, c22])]
    )
    return adj / det


def normal_six(point_jac):
    pairs = [(0, 0), (0, 1), (0, 2), (1, 1), (1, 2), (2, 2)]
    return jnp.stack(
        [jnp.sum(point_jac[:, first] * point_jac[:, second], axis=0) for first, second in pairs]
    )


def expand_six(six):
    return jnp.stack(
        [
            jnp.stack([six[0], six[1], six[2]]),
            jnp.stack([six[1], six[3], six[4]]),
            jnp.stack([six[2], six[4], six[5]]),
        ]
    )


def point_inverse(six, damp):
    mat = expand_six(six) + damp[None, None, :] * jnp.eye(3, dtype=jnp.float32)[:, :, None]
    return invert3(mat)


SIZES = {}


def allsum(value, axis):
    size = SIZES[axis]
    if size == 4 and axis == "one_round":
        peers = [
            lax.ppermute(value, axis, [(i, i ^ mask) for i in range(size)]) for mask in (1, 2, 3)
        ]
        return (value + peers[0]) + (peers[1] + peers[2])
    if size & (size - 1):
        return lax.psum(value, axis)
    step = 1
    while step < size:
        value = value + lax.ppermute(value, axis, [(i, i ^ step) for i in range(size)])
        step *= 2
    return value


def norm_sum(value):
    return allsum(value, "cam")


def on_device(cam_jac, point_jac, obs_cam, obs_point, point_damp, cam_damp, reduced_rhs):
    npts = point_damp.shape[0]
    ncam = reduced_rhs.shape[1]
    by_point = Index(obs_point, npts)
    by_cam = Index(obs_cam, ncam)
    six_terms = allsum(by_point.segsum(normal_six(point_jac)), "cam")
    inv = point_inverse(six_terms, point_damp)
    diag_terms = by_cam.segsum(jnp.sum(cam_jac * cam_jac, axis=0))
    cam_diag = allsum(diag_terms, "pts") + cam_damp[None, :]

    def as_row(rows, width):
        flat = rows.reshape(-1)
        count = -(-flat.shape[0] // width)
        return jnp.pad(flat, (0, count * width - flat.shape[0])).reshape(count, width)

    def lanes(terms):
        return jnp.sum(terms.reshape(-1, ncam), axis=0)

    def operate(vec, extras):
        y = jnp.sum(cam_jac * by_cam.gather(vec)[None], axis=1)
        u_part = by_point.segsum(jnp.sum(point_jac * y[:, None, :], axis=0))
        extras = jnp.stack([lanes(t) for t in extras] + [lanes(cam_damp[None, :] * vec * vec), lanes(y * y)])
        count = extras.shape[0]
        rows = as_row(extras, npts)
        u_all = allsum(jnp.concatenate([u_part, rows], axis=0), "cam")
        u = u_all[:3]
        got = jnp.sum(u_all[3:].reshape(-1)[: count * ncam].reshape(count, ncam), axis=1, keepdims=True)
        w = jnp.sum(inv * u[None, :, :], axis=1)
        pt_terms = jnp.sum(u * w, axis=0).reshape(-1, ncam)
        pt_row = u_all[3:].reshape(-1)[(count - 1) * ncam : count * ncam] - jnp.sum(pt_terms, axis=0)
        z = y - jnp.sum(point_jac * by_point.gather(w)[None], axis=1)
        img_part = by_cam.segsum(jnp.sum(cam_jac * z[:, None, :], axis=0))
        img_all = allsum(jnp.concatenate([img_part, pt_row[None]], axis=0), "pts")
        image = cam_damp[None, :] * vec + img_all[:-1]
        energy = got[count - 2 : count - 1] + jnp.sum(img_all[-1:], axis=1, keepdims=True)
        return image, got, energy

    solution = jnp.zeros_like(reduced_rhs)
    residual = reduced_rhs
    pre = residual / cam_diag
    direction = pre
    image, got, curv = operate(direction, [residual * pre])
    rz = got[0:1]
    alpha = rz / curv
    solution = solution + alpha * direction
    residual = residual - alpha * image
    for step in range(1, ITERS):
        pre = residual / cam_diag
        image_pre, got, energy = operate(pre, [residual * pre, pre * image])
        new_rz = got[0:1]
        beta = new_rz / rz
        direction = pre + beta * direction
        image = image_pre + beta * image
        curv = energy + beta * (2.0 * got[1:2] + beta * curv)
        alpha = new_rz / curv
        rz = new_rz
        solution = solution + alpha * direction
        residual = residual - alpha * image
    return (solution, residual)


def solution(mesh):
    SIZES.update(mesh.shape)
    return jax.shard_map(
        on_device,
        mesh=mesh,
        in_specs=(
            P(None, None, ("groups", "pts", "cam")),
            P(None, None, ("groups", "pts", "cam")),
            P(("groups", "pts", "cam")),
            P(("groups", "pts", "cam")),
            P(("groups", "pts")),
            P(("groups", "cam")),
            P(None, ("groups", "cam")),
        ),
        out_specs=(P(None, ("groups", "cam")), P(None, ("groups", "cam"))),
        check_vma=False,
    )
```

```python
import jax
import jax.numpy as jnp
from jax import lax
from jax.sharding import PartitionSpec as P

ITERS = 3

BF = jnp.bfloat16
F32 = jnp.float32


def split_of(count):
    lo = 1 << max((count.bit_length() - 1) // 2 - 1, 0)
    while count % lo:
        lo //= 2
    return count // lo, lo


def pieces(value):
    first = lax.reduce_precision(value, exponent_bits=8, mantissa_bits=7)
    rest = value - first
    second = lax.reduce_precision(rest, exponent_bits=8, mantissa_bits=7)
    third = rest - second
    return first.astype(BF), second.astype(BF), third.astype(BF)


class Index:
    def __init__(self, index, count):
        self.count = count
        self.hi, self.lo = split_of(count)
        high = index // self.lo
        low = index % self.lo
        hot = (lax.broadcasted_iota(jnp.int32, (self.hi, index.shape[0]), 0) == high[None, :])
        self.hot = hot.astype(BF)
        self.hot3 = jnp.concatenate([self.hot] * 3, axis=1)
        self.hot3t = jnp.concatenate([self.hot] * 3, axis=0)
        self.low = lax.broadcasted_iota(jnp.int32, (self.lo, index.shape[0]), 0) == low[None, :]

    def segsum(self, terms):
        ncol = terms.shape[0]
        parts = [
            jnp.where(self.low[None], part[:, None, :], jnp.zeros((), BF)).reshape(ncol * self.lo, -1)
            for part in pieces(terms)
        ]
        spread = jnp.concatenate(parts, axis=1)
        out = lax.dot_general(
            self.hot3, spread, (((1,), (1,)), ((), ())), preferred_element_type=F32
        )
        return out.reshape(self.hi, ncol, self.lo).transpose(1, 0, 2).reshape(ncol, self.count)

    def gather(self, table):
        ncol = table.shape[0]
        mat = table.reshape(ncol, self.hi, self.lo).transpose(0, 2, 1).reshape(ncol * self.lo, self.hi)
        stacked = jnp.concatenate(pieces(mat), axis=1)
        spread = lax.dot_general(
            stacked, self.hot3t, (((1,), (0,)), ((), ())), preferred_element_type=F32
        ).reshape(ncol, self.lo, -1)
        return jnp.sum(jnp.where(self.low[None], spread, 0.0), axis=1)


def invert3(mat):
    c00 = mat[1, 1] * mat[2, 2] - mat[1, 2] * mat[2, 1]
    c01 = mat[0, 2] * mat[2, 1] - mat[0, 1] * mat[2, 2]
    c02 = mat[0, 1] * mat[1, 2] - mat[0, 2] * mat[1, 1]
    c10 = mat[1, 2] * mat[2, 0] - mat[1, 0] * mat[2, 2]
    c11 = mat[0, 0] * mat[2, 2] - mat[0, 2] * mat[2, 0]
    c12 = mat[0, 2] * mat[1, 0] - mat[0, 0] * mat[1, 2]
    c20 = mat[1, 0] * mat[2, 1] - mat[1, 1] * mat[2, 0]
    c21 = mat[0, 1] * mat[2, 0] - mat[0, 0] * mat[2, 1]
    c22 = mat[0, 0] * mat[1, 1] - mat[0, 1] * mat[1, 0]
    det = mat[0, 0] * c00 + mat[0, 1] * c10 + mat[0, 2] * c20
    adj = jnp.stack(
        [jnp.stack([c00, c01, c02]), jnp.stack([c10, c11, c12]), jnp.stack([c20, c21, c22])]
    )
    return adj / det


def normal_six(point_jac):
    pairs = [(0, 0), (0, 1), (0, 2), (1, 1), (1, 2), (2, 2)]
    return jnp.stack(
        [jnp.sum(point_jac[:, first] * point_jac[:, second], axis=0) for first, second in pairs]
    )


def expand_six(six):
    return jnp.stack(
        [
            jnp.stack([six[0], six[1], six[2]]),
            jnp.stack([six[1], six[3], six[4]]),
            jnp.stack([six[2], six[4], six[5]]),
        ]
    )


def point_inverse(six, damp):
    mat = expand_six(six) + damp[None, None, :] * jnp.eye(3, dtype=jnp.float32)[:, :, None]
    return invert3(mat)


SIZES = {}


def allsum(value, axis):
    size = SIZES[axis]
    if size == 4 and axis == "one_round":
        peers = [
            lax.ppermute(value, axis, [(i, i ^ mask) for i in range(size)]) for mask in (1, 2, 3)
        ]
        return (value + peers[0]) + (peers[1] + peers[2])
    if size & (size - 1):
        return lax.psum(value, axis)
    step = size // 2 if axis == "pts" else 1
    while 0 < step < size:
        value = value + lax.ppermute(value, axis, [(i, i ^ step) for i in range(size)])
        step = step // 2 if axis == "pts" else step * 2
    return value


def norm_sum(value):
    return allsum(value, "cam")


def on_device(cam_jac, point_jac, obs_cam, obs_point, point_damp, cam_damp, reduced_rhs):
    npts = point_damp.shape[0]
    ncam = reduced_rhs.shape[1]
    by_point = Index(obs_point, npts)
    by_cam = Index(obs_cam, ncam)
    six_terms = allsum(by_point.segsum(normal_six(point_jac)), "cam")
    inv = point_inverse(six_terms, point_damp)
    diag_terms = by_cam.segsum(jnp.sum(cam_jac * cam_jac, axis=0))
    cam_diag = allsum(diag_terms, "pts") + cam_damp[None, :]

    def as_row(rows, width):
        flat = rows.reshape(-1)
        count = -(-flat.shape[0] // width)
        return jnp.pad(flat, (0, count * width - flat.shape[0])).reshape(count, width)

    def lanes(terms):
        return jnp.sum(terms.reshape(-1, ncam), axis=0)

    def operate(vec, extras):
        y = jnp.sum(cam_jac * by_cam.gather(vec)[None], axis=1)
        u_part = by_point.segsum(jnp.sum(point_jac * y[:, None, :], axis=0))
        extras = jnp.stack([lanes(t) for t in extras] + [lanes(cam_damp[None, :] * vec * vec), lanes(y * y)])
        count = extras.shape[0]
        rows = as_row(extras, npts)
        u_all = allsum(jnp.concatenate([u_part, rows], axis=0), "cam")
        u = u_all[:3]
        got = jnp.sum(u_all[3:].reshape(-1)[: count * ncam].reshape(count, ncam), axis=1, keepdims=True)
        w = jnp.sum(inv * u[None, :, :], axis=1)
        pt_terms = jnp.sum(u * w, axis=0).reshape(-1, ncam)
        pt_row = u_all[3:].reshape(-1)[(count - 1) * ncam : count * ncam] - jnp.sum(pt_terms, axis=0)
        z = y - jnp.sum(point_jac * by_point.gather(w)[None], axis=1)
        img_part = by_cam.segsum(jnp.sum(cam_jac * z[:, None, :], axis=0))
        img_all = allsum(jnp.concatenate([img_part, pt_row[None]], axis=0), "pts")
        image = cam_damp[None, :] * vec + img_all[:-1]
        energy = got[count - 2 : count - 1] + jnp.sum(img_all[-1:], axis=1, keepdims=True)
        return image, got, energy

    solution = jnp.zeros_like(reduced_rhs)
    residual = reduced_rhs
    pre = residual / cam_diag
    direction = pre
    image, got, curv = operate(direction, [residual * pre])
    rz = got[0:1]
    alpha = rz / curv
    solution = solution + alpha * direction
    residual = residual - alpha * image
    for step in range(1, ITERS):
        pre = residual / cam_diag
        image_pre, got, energy = operate(pre, [residual * pre, pre * image])
        new_rz = got[0:1]
        beta = new_rz / rz
        direction = pre + beta * direction
        image = image_pre + beta * image
        curv = energy + beta * (2.0 * got[1:2] + beta * curv)
        alpha = new_rz / curv
        rz = new_rz
        solution = solution + alpha * direction
        residual = residual - alpha * image
    return (solution, residual)


def solution(mesh):
    SIZES.update(mesh.shape)
    return jax.shard_map(
        on_device,
        mesh=mesh,
        in_specs=(
            P(None, None, ("groups", "pts", "cam")),
            P(None, None, ("groups", "pts", "cam")),
            P(("groups", "pts", "cam")),
            P(("groups", "pts", "cam")),
            P(("groups", "pts")),
            P(("groups", "cam")),
            P(None, ("groups", "cam")),
        ),
        out_specs=(P(None, ("groups", "cam")), P(None, ("groups", "cam"))),
        check_vma=False,
    )
```

```python
import jax
import jax.numpy as jnp
from jax import lax
from jax.sharding import PartitionSpec as P

ITERS = 3

BF = jnp.bfloat16
F32 = jnp.float32


def split_of(count):
    lo = 1 << max((count.bit_length() - 1) // 2 - 1, 0)
    while count % lo:
        lo //= 2
    return count // lo, lo


def pieces(value):
    first = lax.reduce_precision(value, exponent_bits=8, mantissa_bits=7)
    rest = value - first
    second = lax.reduce_precision(rest, exponent_bits=8, mantissa_bits=7)
    third = rest - second
    return first.astype(BF), second.astype(BF), third.astype(BF)


class Index:
    def __init__(self, index, count):
        self.count = count
        self.hi, self.lo = split_of(count)
        high = index // self.lo
        low = index % self.lo
        hot = (lax.broadcasted_iota(jnp.int32, (self.hi, index.shape[0]), 0) == high[None, :])
        self.hot = hot.astype(BF)
        self.hot3 = jnp.concatenate([self.hot] * 3, axis=1)
        self.hot3t = jnp.concatenate([self.hot] * 3, axis=0)
        self.low = lax.broadcasted_iota(jnp.int32, (self.lo, index.shape[0]), 0) == low[None, :]

    def segsum(self, terms):
        ncol = terms.shape[0]
        parts = [
            jnp.where(self.low[None], part[:, None, :], jnp.zeros((), BF)).reshape(ncol * self.lo, -1)
            for part in pieces(terms)
        ]
        spread = jnp.concatenate(parts, axis=1)
        out = lax.dot_general(
            self.hot3, spread, (((1,), (1,)), ((), ())), preferred_element_type=F32
        )
        return out.reshape(self.hi, ncol, self.lo).transpose(1, 0, 2).reshape(ncol, self.count)

    def gather(self, table):
        ncol = table.shape[0]
        mat = table.reshape(ncol, self.hi, self.lo).transpose(0, 2, 1).reshape(ncol * self.lo, self.hi)
        stacked = jnp.concatenate(pieces(mat), axis=1)
        spread = lax.dot_general(
            stacked, self.hot3t, (((1,), (0,)), ((), ())), preferred_element_type=F32
        ).reshape(ncol, self.lo, -1)
        return jnp.sum(jnp.where(self.low[None], spread, 0.0), axis=1)


def invert3(mat):
    c00 = mat[1, 1] * mat[2, 2] - mat[1, 2] * mat[2, 1]
    c01 = mat[0, 2] * mat[2, 1] - mat[0, 1] * mat[2, 2]
    c02 = mat[0, 1] * mat[1, 2] - mat[0, 2] * mat[1, 1]
    c10 = mat[1, 2] * mat[2, 0] - mat[1, 0] * mat[2, 2]
    c11 = mat[0, 0] * mat[2, 2] - mat[0, 2] * mat[2, 0]
    c12 = mat[0, 2] * mat[1, 0] - mat[0, 0] * mat[1, 2]
    c20 = mat[1, 0] * mat[2, 1] - mat[1, 1] * mat[2, 0]
    c21 = mat[0, 1] * mat[2, 0] - mat[0, 0] * mat[2, 1]
    c22 = mat[0, 0] * mat[1, 1] - mat[0, 1] * mat[1, 0]
    det = mat[0, 0] * c00 + mat[0, 1] * c10 + mat[0, 2] * c20
    adj = jnp.stack(
        [jnp.stack([c00, c01, c02]), jnp.stack([c10, c11, c12]), jnp.stack([c20, c21, c22])]
    )
    return adj / det


def normal_six(point_jac):
    pairs = [(0, 0), (0, 1), (0, 2), (1, 1), (1, 2), (2, 2)]
    return jnp.stack(
        [jnp.sum(point_jac[:, first] * point_jac[:, second], axis=0) for first, second in pairs]
    )


def expand_six(six):
    return jnp.stack(
        [
            jnp.stack([six[0], six[1], six[2]]),
            jnp.stack([six[1], six[3], six[4]]),
            jnp.stack([six[2], six[4], six[5]]),
        ]
    )


def point_inverse(six, damp):
    mat = expand_six(six) + damp[None, None, :] * jnp.eye(3, dtype=jnp.float32)[:, :, None]
    return invert3(mat)


SIZES = {}


def allsum(value, axis):
    size = SIZES[axis]
    if size == 4 and axis == "one_round":
        peers = [
            lax.ppermute(value, axis, [(i, i ^ mask) for i in range(size)]) for mask in (1, 2, 3)
        ]
        return (value + peers[0]) + (peers[1] + peers[2])
    if size & (size - 1):
        return lax.psum(value, axis)
    step = size // 2 if axis == "cam" else 1
    while 0 < step < size:
        value = value + lax.ppermute(value, axis, [(i, i ^ step) for i in range(size)])
        step = step // 2 if axis == "cam" else step * 2
    return value


def norm_sum(value):
    return allsum(value, "cam")


def on_device(cam_jac, point_jac, obs_cam, obs_point, point_damp, cam_damp, reduced_rhs):
    npts = point_damp.shape[0]
    ncam = reduced_rhs.shape[1]
    by_point = Index(obs_point, npts)
    by_cam = Index(obs_cam, ncam)
    six_terms = allsum(by_point.segsum(normal_six(point_jac)), "cam")
    inv = point_inverse(six_terms, point_damp)
    diag_terms = by_cam.segsum(jnp.sum(cam_jac * cam_jac, axis=0))
    cam_diag = allsum(diag_terms, "pts") + cam_damp[None, :]

    def as_row(rows, width):
        flat = rows.reshape(-1)
        count = -(-flat.shape[0] // width)
        return jnp.pad(flat, (0, count * width - flat.shape[0])).reshape(count, width)

    def lanes(terms):
        return jnp.sum(terms.reshape(-1, ncam), axis=0)

    def operate(vec, extras):
        y = jnp.sum(cam_jac * by_cam.gather(vec)[None], axis=1)
        u_part = by_point.segsum(jnp.sum(point_jac * y[:, None, :], axis=0))
        extras = jnp.stack([lanes(t) for t in extras] + [lanes(cam_damp[None, :] * vec * vec), lanes(y * y)])
        count = extras.shape[0]
        rows = as_row(extras, npts)
        u_all = allsum(jnp.concatenate([u_part, rows], axis=0), "cam")
        u = u_all[:3]
        got = jnp.sum(u_all[3:].reshape(-1)[: count * ncam].reshape(count, ncam), axis=1, keepdims=True)
        w = jnp.sum(inv * u[None, :, :], axis=1)
        pt_terms = jnp.sum(u * w, axis=0).reshape(-1, ncam)
        pt_row = u_all[3:].reshape(-1)[(count - 1) * ncam : count * ncam] - jnp.sum(pt_terms, axis=0)
        z = y - jnp.sum(point_jac * by_point.gather(w)[None], axis=1)
        img_part = by_cam.segsum(jnp.sum(cam_jac * z[:, None, :], axis=0))
        img_all = allsum(jnp.concatenate([img_part, pt_row[None]], axis=0), "pts")
        image = cam_damp[None, :] * vec + img_all[:-1]
        energy = got[count - 2 : count - 1] + jnp.sum(img_all[-1:], axis=1, keepdims=True)
        return image, got, energy

    solution = jnp.zeros_like(reduced_rhs)
    residual = reduced_rhs
    pre = residual / cam_diag
    direction = pre
    image, got, curv = operate(direction, [residual * pre])
    rz = got[0:1]
    alpha = rz / curv
    solution = solution + alpha * direction
    residual = residual - alpha * image
    for step in range(1, ITERS):
        pre = residual / cam_diag
        image_pre, got, energy = operate(pre, [residual * pre, pre * image])
        new_rz = got[0:1]
        beta = new_rz / rz
        direction = pre + beta * direction
        image = image_pre + beta * image
        curv = energy + beta * (2.0 * got[1:2] + beta * curv)
        alpha = new_rz / curv
        rz = new_rz
        solution = solution + alpha * direction
        residual = residual - alpha * image
    return (solution, residual)


def solution(mesh):
    SIZES.update(mesh.shape)
    return jax.shard_map(
        on_device,
        mesh=mesh,
        in_specs=(
            P(None, None, ("groups", "pts", "cam")),
            P(None, None, ("groups", "pts", "cam")),
            P(("groups", "pts", "cam")),
            P(("groups", "pts", "cam")),
            P(("groups", "pts")),
            P(("groups", "cam")),
            P(None, ("groups", "cam")),
        ),
        out_specs=(P(None, ("groups", "cam")), P(None, ("groups", "cam"))),
        check_vma=False,
    )
```

```python
import jax
import jax.numpy as jnp
from jax import lax
from jax.sharding import PartitionSpec as P

ITERS = 3

BF = jnp.bfloat16
F32 = jnp.float32


def split_of(count):
    lo = 1 << max((count.bit_length() - 1) // 2 - 1, 0)
    while count % lo:
        lo //= 2
    return count // lo, lo


def pieces(value):
    first = lax.reduce_precision(value, exponent_bits=8, mantissa_bits=7)
    rest = value - first
    second = lax.reduce_precision(rest, exponent_bits=8, mantissa_bits=7)
    third = rest - second
    return first.astype(BF), second.astype(BF), third.astype(BF)


class Index:
    def __init__(self, index, count):
        self.count = count
        self.hi, self.lo = split_of(count)
        high = index // self.lo
        low = index % self.lo
        hot = (lax.broadcasted_iota(jnp.int32, (self.hi, index.shape[0]), 0) == high[None, :])
        self.hot = hot.astype(BF)
        self.hot3 = jnp.concatenate([self.hot] * 3, axis=1)
        self.hot3t = jnp.concatenate([self.hot] * 3, axis=0)
        self.low = lax.broadcasted_iota(jnp.int32, (self.lo, index.shape[0]), 0) == low[None, :]

    def segsum(self, terms):
        ncol = terms.shape[0]
        parts = [
            jnp.where(self.low[None], part[:, None, :], jnp.zeros((), BF)).reshape(ncol * self.lo, -1)
            for part in pieces(terms)
        ]
        spread = jnp.concatenate(parts, axis=1)
        out = lax.dot_general(
            self.hot3, spread, (((1,), (1,)), ((), ())), preferred_element_type=F32
        )
        return out.reshape(self.hi, ncol, self.lo).transpose(1, 0, 2).reshape(ncol, self.count)

    def gather(self, table):
        ncol = table.shape[0]
        mat = table.reshape(ncol, self.hi, self.lo).transpose(0, 2, 1).reshape(ncol * self.lo, self.hi)
        stacked = jnp.concatenate(pieces(mat), axis=1)
        spread = lax.dot_general(
            stacked, self.hot3t, (((1,), (0,)), ((), ())), preferred_element_type=F32
        ).reshape(ncol, self.lo, -1)
        return jnp.sum(jnp.where(self.low[None], spread, 0.0), axis=1)


def invert3(mat):
    c00 = mat[1, 1] * mat[2, 2] - mat[1, 2] * mat[2, 1]
    c01 = mat[0, 2] * mat[2, 1] - mat[0, 1] * mat[2, 2]
    c02 = mat[0, 1] * mat[1, 2] - mat[0, 2] * mat[1, 1]
    c10 = mat[1, 2] * mat[2, 0] - mat[1, 0] * mat[2, 2]
    c11 = mat[0, 0] * mat[2, 2] - mat[0, 2] * mat[2, 0]
    c12 = mat[0, 2] * mat[1, 0] - mat[0, 0] * mat[1, 2]
    c20 = mat[1, 0] * mat[2, 1] - mat[1, 1] * mat[2, 0]
    c21 = mat[0, 1] * mat[2, 0] - mat[0, 0] * mat[2, 1]
    c22 = mat[0, 0] * mat[1, 1] - mat[0, 1] * mat[1, 0]
    det = mat[0, 0] * c00 + mat[0, 1] * c10 + mat[0, 2] * c20
    adj = jnp.stack(
        [jnp.stack([c00, c01, c02]), jnp.stack([c10, c11, c12]), jnp.stack([c20, c21, c22])]
    )
    return adj / det


def normal_six(point_jac):
    pairs = [(0, 0), (0, 1), (0, 2), (1, 1), (1, 2), (2, 2)]
    return jnp.stack(
        [jnp.sum(point_jac[:, first] * point_jac[:, second], axis=0) for first, second in pairs]
    )


def expand_six(six):
    return jnp.stack(
        [
            jnp.stack([six[0], six[1], six[2]]),
            jnp.stack([six[1], six[3], six[4]]),
            jnp.stack([six[2], six[4], six[5]]),
        ]
    )


def point_inverse(six, damp):
    mat = expand_six(six) + damp[None, None, :] * jnp.eye(3, dtype=jnp.float32)[:, :, None]
    return invert3(mat)


SIZES = {}


def allsum(value, axis):
    size = SIZES[axis]
    if size == 4 and axis == "one_round":
        peers = [
            lax.ppermute(value, axis, [(i, i ^ mask) for i in range(size)]) for mask in (1, 2, 3)
        ]
        return (value + peers[0]) + (peers[1] + peers[2])
    if size & (size - 1):
        return lax.psum(value, axis)
    step = size // 2
    while 0 < step < size:
        value = value + lax.ppermute(value, axis, [(i, i ^ step) for i in range(size)])
        step = step // 2
    return value


def norm_sum(value):
    return allsum(value, "cam")


def on_device(cam_jac, point_jac, obs_cam, obs_point, point_damp, cam_damp, reduced_rhs):
    npts = point_damp.shape[0]
    ncam = reduced_rhs.shape[1]
    by_point = Index(obs_point, npts)
    by_cam = Index(obs_cam, ncam)
    six_terms = allsum(by_point.segsum(normal_six(point_jac)), "cam")
    inv = point_inverse(six_terms, point_damp)
    diag_terms = by_cam.segsum(jnp.sum(cam_jac * cam_jac, axis=0))
    cam_diag = allsum(diag_terms, "pts") + cam_damp[None, :]

    def as_row(rows, width):
        flat = rows.reshape(-1)
        count = -(-flat.shape[0] // width)
        return jnp.pad(flat, (0, count * width - flat.shape[0])).reshape(count, width)

    def lanes(terms):
        return jnp.sum(terms.reshape(-1, ncam), axis=0)

    def operate(vec, extras):
        y = jnp.sum(cam_jac * by_cam.gather(vec)[None], axis=1)
        u_part = by_point.segsum(jnp.sum(point_jac * y[:, None, :], axis=0))
        extras = jnp.stack([lanes(t) for t in extras] + [lanes(cam_damp[None, :] * vec * vec), lanes(y * y)])
        count = extras.shape[0]
        rows = as_row(extras, npts)
        u_all = allsum(jnp.concatenate([u_part, rows], axis=0), "cam")
        u = u_all[:3]
        got = jnp.sum(u_all[3:].reshape(-1)[: count * ncam].reshape(count, ncam), axis=1, keepdims=True)
        w = jnp.sum(inv * u[None, :, :], axis=1)
        pt_terms = jnp.sum(u * w, axis=0).reshape(-1, ncam)
        pt_row = u_all[3:].reshape(-1)[(count - 1) * ncam : count * ncam] - jnp.sum(pt_terms, axis=0)
        z = y - jnp.sum(point_jac * by_point.gather(w)[None], axis=1)
        img_part = by_cam.segsum(jnp.sum(cam_jac * z[:, None, :], axis=0))
        img_all = allsum(jnp.concatenate([img_part, pt_row[None]], axis=0), "pts")
        image = cam_damp[None, :] * vec + img_all[:-1]
        energy = got[count - 2 : count - 1] + jnp.sum(img_all[-1:], axis=1, keepdims=True)
        return image, got, energy

    solution = jnp.zeros_like(reduced_rhs)
    residual = reduced_rhs
    pre = residual / cam_diag
    direction = pre
    image, got, curv = operate(direction, [residual * pre])
    rz = got[0:1]
    alpha = rz / curv
    solution = solution + alpha * direction
    residual = residual - alpha * image
    for step in range(1, ITERS):
        pre = residual / cam_diag
        image_pre, got, energy = operate(pre, [residual * pre, pre * image])
        new_rz = got[0:1]
        beta = new_rz / rz
        direction = pre + beta * direction
        image = image_pre + beta * image
        curv = energy + beta * (2.0 * got[1:2] + beta * curv)
        alpha = new_rz / curv
        rz = new_rz
        solution = solution + alpha * direction
        residual = residual - alpha * image
    return (solution, residual)


def solution(mesh):
    SIZES.update(mesh.shape)
    return jax.shard_map(
        on_device,
        mesh=mesh,
        in_specs=(
            P(None, None, ("groups", "pts", "cam")),
            P(None, None, ("groups", "pts", "cam")),
            P(("groups", "pts", "cam")),
            P(("groups", "pts", "cam")),
            P(("groups", "pts")),
            P(("groups", "cam")),
            P(None, ("groups", "cam")),
        ),
        out_specs=(P(None, ("groups", "cam")), P(None, ("groups", "cam"))),
        check_vma=False,
    )
```
